32 devices in a mesh: row: 4 (over z), col: 8 (over y, x, core).
Axes of the slice: x: 2, y: 2, z: 4, core: 2. Of those that a mesh axis runs over, the one named last changes fastest.
Arguments:
- covariance: float32 [8192, 8192], P('row', 'col'), as said below
- self_block: bfloat16 [8192, 512], P(('row', 'col')), may hold values from -0.25 to 0.25
- wake_block: bfloat16 [16, 4, 128, 128], replicated, may hold values from -0.375 to 0.375
- upstream: int32 [16, 4], replicated, may hold values from -1 to 15, as said below
- process_noise: float32 [8192], P('col'), may hold values from 0.5 to 2
- sensor_turbine: int32 [384], replicated, may hold values from 0 to 15
- azimuth_index: int32 [16], replicated, may hold values from 0 to 71
- sensor_weight: float32 [384, 512], replicated, may hold values from -0.25 to 0.25
- sensor_noise: float32 [384], replicated, may hold values from 0.5 to 2
Outputs:
- posterior: float32 [8192, 8192], P('row', 'col')
- kalman_gain: float32 [8192, 384], P('row', 'col')
The draws below stay inside these ranges and needn't reach their ends.
Inputs may be any that keep to these rules, and one draw needn't show every extreme that they name: Row t lists distinct turbines other than t that lie upstream of t, valid entries first, then -1; some turbine lists 4. `covariance`: symmetric and positive definite.
All inputs are finite; a program needn't handle non-finite values.
Results may differ from the reference program's by a relative error of at most 0.0048.
Values may be sent and summed in bfloat16 or wider, within the bound.
No kernel may reach another device: no remote copies, remote signals or barrier semaphores. Data moves between devices by JAX's collectives and lax.ppermute only.
A program may use at most 128 MiB of HBM per device.

```python
import math
import jax
import jax.numpy as jnp
from jax import lax

TURB = 16
SPT = 512
INF = 128
SENS = 384
NUP = 4
NAZ = 72
STATES = 8192


def draw_covariance(key, part):
    count = TURB * SPT
    key_factor, key_diag = jax.random.split(key, 2)
    index = jnp.arange(count)
    factor = jax.random.normal(key_factor, (count, count), jnp.float32)
    gram = jnp.dot(factor, factor.T, precision=lax.Precision.HIGHEST) * jnp.float32(1.0 / count)
    gram = 0.5 * (gram + gram.T)
    diagonal = jax.random.uniform(key_diag, (count,), jnp.float32, 1.0, 3.0)
    return gram + jnp.where(index[:, None] == index[None, :], diagonal[:, None], jnp.float32(0.0))


def draw_upstream(key, part):
    key_order, key_count = jax.random.split(key)
    ordering = jax.random.permutation(key_order, TURB)
    position = jnp.argsort(ordering, stable=True)
    counts = jax.random.randint(key_count, (TURB,), 0, NUP + 1)
    counts = jnp.minimum(counts, position)
    counts = jnp.where(position == TURB - 1, NUP, counts)
    slot_ids = jnp.arange(NUP)
    source_position = jnp.clip(position[:, None] - 1 - slot_ids[None, :], 0, TURB - 1)
    sources = ordering[source_position]
    return jnp.where(slot_ids[None, :] < counts[:, None], sources, -1).astype(jnp.int32)


def with_ends(entries, rng, least, top_value):
    spot = [jax.random.randint(jax.random.fold_in(rng, axis), (), 0, length) for axis, length in enumerate(entries.shape)]
    widest = entries.shape.index(max(entries.shape))
    next_to = spot[:widest] + [(spot[widest] + 1) % entries.shape[widest]] + spot[widest + 1:]
    return entries.at[tuple(spot)].set(least).at[tuple(next_to)].set(top_value)


def block_scale(key, dims, cuts, smallest, top_value):
    gain = 1.0
    for dim, parts in cuts:
        draws = jax.random.uniform(jax.random.fold_in(jax.random.fold_in(key, 6), dim), (parts,), jnp.float32, smallest / len(cuts), top_value / len(cuts))
        gain = gain * jnp.repeat(jnp.exp(draws), dims[dim] // parts).reshape((-1,) + (1,) * (len(dims) - 1 - dim))
    return gain


def normal_values(stream_key, shape, spread, limit, cuts=(), held_as=jnp.bfloat16):
    drawn = jax.random.normal(stream_key, shape, jnp.float32) * spread
    if len(cuts) > 0:
        drawn = block_scale(stream_key, shape, cuts, -0.22, 0.18) * drawn
    return jnp.clip(drawn, min=-limit, max=limit).astype(held_as)


def setup_inputs(seed: int = 0) -> dict:
    key_list = jax.random.split(jax.random.key(seed), 10)
    return {
        "covariance": draw_covariance(jax.random.fold_in(key_list[9], 71), 0),
        "self_block": normal_values(key_list[1], (STATES, SPT), SPT ** -0.5, 0.25, ((0, 32),)),
        "wake_block": normal_values(key_list[2], (TURB, NUP, INF, INF), (2 * INF) ** -0.5, 0.375),
        "upstream": draw_upstream(jax.random.fold_in(key_list[9], 71), 0),
        "process_noise": jnp.clip(jnp.exp(math.log(2.0) - 1.3862944 * jax.random.uniform(key_list[4], (STATES,), jnp.float32) ** block_scale(key_list[4], (STATES,), ((0, 8),), -0.2, 0.2)), 0.5, 2.0),
        "sensor_turbine": with_ends(jax.random.randint(key_list[5], (SENS,), 0, TURB), jax.random.fold_in(key_list[5], 1), 0, TURB - 1).astype(jnp.int32),
        "azimuth_index": with_ends(jax.random.randint(key_list[6], (TURB,), 0, NAZ), jax.random.fold_in(key_list[6], 1), 0, NAZ - 1).astype(jnp.int32),
        "sensor_weight": normal_values(key_list[7], (SENS, SPT), SPT ** -0.5, 0.25, (), jnp.float32),
        "sensor_noise": jnp.clip(jnp.exp(jax.random.uniform(key_list[8], (SENS,), jnp.float32, math.log(0.5), math.log(2.0))), 0.5, 2.0),
    }


def transition_apply(source, self_block, wake_block, upstream):
    width = source.shape[1]
    results = []
    for turbine in range(TURB):
        own_rows = self_block[turbine * SPT:(turbine + 1) * SPT].astype(jnp.float32)
        own_source = source[turbine * SPT:(turbine + 1) * SPT].astype(jnp.float32)
        result = jnp.dot(own_rows, own_source, precision=lax.Precision.HIGHEST)
        inflow_sum = jnp.zeros((INF, width), jnp.float32)
        for slot_index in range(NUP):
            anchor = upstream[turbine, slot_index]
            start_row = (jnp.maximum(anchor, 0) * SPT).astype(jnp.int32)
            piece = lax.dynamic_slice_in_dim(source, start_row, INF, 0).astype(jnp.float32)
            coupling = wake_block[turbine, slot_index].astype(jnp.float32)
            term = jnp.dot(coupling, piece, precision=lax.Precision.HIGHEST)
            inflow_sum = inflow_sum + jnp.where(anchor >= 0, term, jnp.float32(0.0))
        result = result + jnp.concatenate([inflow_sum, jnp.zeros((SPT - INF, width), jnp.float32)], 0)
        results.append(result)
    return jnp.concatenate(results, 0)

def reference(covariance, self_block, wake_block, upstream, process_noise, sensor_turbine, azimuth_index, sensor_weight, sensor_noise):
    half_product = transition_apply(covariance, self_block, wake_block, upstream).astype(jnp.bfloat16)
    predicted = transition_apply(half_product.T, self_block, wake_block, upstream).T
    predicted = predicted + jnp.diag(process_noise)
    sensor_index = jnp.arange(SENS)
    blade_angle = azimuth_index[sensor_turbine].astype(jnp.float32) * jnp.float32(2.0 * math.pi / NAZ) + (sensor_index % 3).astype(jnp.float32) * jnp.float32(2.0 * math.pi / 3.0)
    offset = jnp.arange(SPT)
    cosine = jnp.cos(blade_angle)[:, None]
    sine = jnp.sin(blade_angle)[:, None]
    factor = jnp.where(offset[None, :] < 2 * INF, jnp.float32(1.0), jnp.where(offset[None, :] < 3 * INF, cosine, sine))
    turbine_rows = sensor_weight * factor
    state_turbine = jnp.arange(STATES) // SPT
    observe = jnp.where(sensor_turbine[:, None] == state_turbine[None, :], jnp.tile(turbine_rows, (1, TURB)), jnp.float32(0.0))
    cross_cov = jnp.dot(predicted, observe.T, precision=lax.Precision.HIGHEST)
    innovation = jnp.dot(observe, cross_cov, precision=lax.Precision.HIGHEST) + jnp.diag(sensor_noise)
    symmetric = 0.5 * (innovation + innovation.T)
    lower = jnp.linalg.cholesky(symmetric)
    kalman_gain = jax.scipy.linalg.cho_solve((lower, True), cross_cov.T).T
    posterior = predicted - jnp.dot(kalman_gain, cross_cov.T, precision=lax.Precision.HIGHEST)
    return (posterior, kalman_gain)
```

```python
import math

import jax
import jax.numpy as jnp
from jax import lax
from jax.sharding import PartitionSpec as P

TURB = 16
SPT = 512
INF = 128
NUP = 4
NAZ = 72


def broadcast(value, axis, root):
    mine = lax.axis_index(axis) == root
    return lax.psum(jnp.where(mine, value, jnp.zeros_like(value)), axis)


def observe_columns(sensor_weight, sensor_turbine, azimuth_index, start, count):
    sensors = sensor_weight.shape[0]
    matches = sensor_turbine[:, None] == jnp.arange(TURB)[None, :]
    rotor_index = jnp.sum(jnp.where(matches, azimuth_index[None, :], 0), axis=1)
    sensor_index = jnp.arange(sensors)
    blade_angle = rotor_index.astype(jnp.float32) * jnp.float32(2.0 * math.pi / NAZ) + (
        sensor_index % 3
    ).astype(jnp.float32) * jnp.float32(2.0 * math.pi / 3.0)
    positions = start + jnp.arange(count)
    turbine_of = positions // SPT
    offset_of = positions % SPT
    widened = jnp.tile(sensor_weight, (1, max(1, count // SPT)))
    weights = lax.dynamic_slice_in_dim(widened, start % SPT, count, 1)
    cosine = jnp.cos(blade_angle)[:, None]
    sine = jnp.sin(blade_angle)[:, None]
    factor = jnp.where(
        offset_of[None, :] < 2 * INF,
        jnp.float32(1.0),
        jnp.where(offset_of[None, :] < 3 * INF, cosine, sine),
    )
    return jnp.where(
        sensor_turbine[:, None] == turbine_of[None, :], weights * factor, jnp.float32(0.0)
    )


def split_bf16(x):
    high = x.astype(jnp.bfloat16)
    low = (x - high.astype(jnp.float32)).astype(jnp.bfloat16)
    return high, low


def coupling_matrix(wake_block, upstream, turbine):
    slots = upstream[turbine]
    blocks = jnp.zeros((INF, TURB, INF), jnp.bfloat16)
    for slot_index in range(NUP):
        anchor = slots[slot_index]
        hit = (jnp.arange(TURB) == anchor)[None, :, None]
        blocks = blocks + jnp.where(
            hit, wake_block[turbine, slot_index][:, None, :], jnp.zeros((), jnp.bfloat16)
        )
    return blocks.reshape(INF, TURB * INF)


def dot_f32(a, b, dims):
    return lax.dot_general(a, b, (dims, ((), ())), preferred_element_type=jnp.float32)


def shards(
    covariance,
    self_block,
    wake_block,
    upstream,
    process_noise,
    sensor_turbine,
    azimuth_index,
    sensor_weight,
    sensor_noise,
):
    row_count, col_count = covariance.shape
    row_start = lax.axis_index("row") * row_count
    col_start = lax.axis_index("col") * col_count
    per_row = row_count // SPT
    per_col = max(1, col_count // SPT)
    first_turbine = lax.axis_index("row") * per_row

    cov3 = covariance.reshape(per_row, SPT, col_count)
    inflow_all = lax.all_gather(cov3[:, :INF, :], "row", axis=0, tiled=True)
    inflow_high, inflow_low = split_bf16(inflow_all.reshape(TURB * INF, col_count))
    own_rows = lax.all_gather(self_block, "col", axis=0, tiled=True)
    cov_high, cov_low = split_bf16(cov3)
    blocks = []
    for local in range(per_row):
        turbine = first_turbine + local
        diag_rows = own_rows[local * SPT : (local + 1) * SPT]
        result = dot_f32(diag_rows, cov_high[local], ((1,), (0,))) + dot_f32(
            diag_rows, cov_low[local], ((1,), (0,))
        )
        coupling = coupling_matrix(wake_block, upstream, turbine)
        inflow_sum = dot_f32(coupling, inflow_high, ((1,), (0,))) + dot_f32(
            coupling, inflow_low, ((1,), (0,))
        )
        result = jnp.concatenate([result[:INF] + inflow_sum, result[INF:]], 0)
        blocks.append(result.astype(jnp.bfloat16))
    half_product = jnp.concatenate(blocks, 0)

    if col_count >= SPT:
        half3 = half_product.reshape(row_count, per_col, SPT)
        half_inflow = jnp.transpose(half3[:, :, :INF], (1, 0, 2))
        half_inflow_all = lax.all_gather(half_inflow, "col", axis=0, tiled=True)
        turbine_cols = [half3[:, local, :] for local in range(per_col)]
    else:
        full = lax.all_gather(half_product, "col", axis=1, tiled=True)
        half_inflow_all = jnp.transpose(full.reshape(row_count, TURB, SPT)[:, :, :INF], (1, 0, 2))
        turbine_cols = [lax.dynamic_slice_in_dim(full, (col_start // SPT) * SPT, SPT, 1)]
    target_rows = lax.dynamic_slice_in_dim(own_rows, col_start % row_count, col_count, 0)
    target_rows = broadcast(target_rows, "row", col_start // row_count)
    piece_width = min(col_count, SPT)
    pieces = []
    for local in range(per_col):
        turbine = col_start // SPT + local
        diag_rows = target_rows[local * piece_width : (local + 1) * piece_width]
        result = dot_f32(turbine_cols[local], diag_rows, ((1,), (1,)))
        coupling = coupling_matrix(wake_block, upstream, turbine).reshape(INF, TURB, INF)
        inflow_sum = dot_f32(half_inflow_all, coupling, ((0, 2), (1, 2)))
        inflow_sum = jnp.where(col_start % SPT == 0, inflow_sum, jnp.float32(0.0))
        pieces.append(jnp.concatenate([result[:, :INF] + inflow_sum, result[:, INF:]], 1))
    predicted = jnp.concatenate(pieces, 1)
    row_ids = row_start + jnp.arange(row_count)
    col_ids = col_start + jnp.arange(col_count)
    predicted = predicted + jnp.where(
        row_ids[:, None] == col_ids[None, :], process_noise[None, :], jnp.float32(0.0)
    )

    col_observe = observe_columns(
        sensor_weight, sensor_turbine, azimuth_index, col_start, col_count
    )
    partial_cross = jnp.dot(predicted, col_observe.T, precision=lax.Precision.HIGHEST)
    cross_cov = lax.psum(partial_cross, "col")
    row_observe = observe_columns(
        sensor_weight, sensor_turbine, azimuth_index, row_start, row_count
    )
    partial_innovation = jnp.dot(row_observe, cross_cov, precision=lax.Precision.HIGHEST)
    innovation = lax.psum(partial_innovation, "row") + jnp.diag(sensor_noise)
    symmetric = 0.5 * (innovation + innovation.T)
    lower = jnp.linalg.cholesky(symmetric)
    sensors = symmetric.shape[0]
    lower_inverse = jax.scipy.linalg.solve_triangular(
        lower, jnp.eye(sensors, dtype=jnp.float32), lower=True
    )
    inverse = jnp.dot(lower_inverse.T, lower_inverse, precision=lax.Precision.HIGHEST)
    gain_block = jnp.dot(cross_cov, inverse, precision=lax.Precision.HIGHEST)
    target_cross = lax.dynamic_slice_in_dim(cross_cov, col_start % row_count, col_count, 0)
    target_cross = broadcast(target_cross, "row", col_start // row_count)
    posterior = predicted - jnp.dot(gain_block, target_cross.T, precision=lax.Precision.HIGHEST)
    share = gain_block.shape[1] // lax.axis_size("col")
    gain_share = lax.dynamic_slice_in_dim(gain_block, lax.axis_index("col") * share, share, 1)
    return (posterior, gain_share)


def solution(mesh):
    in_specs = (P("row", "col"), P(("row", "col"), None), P(), P(), P("col"), P(), P(), P(), P())
    out_specs = (P("row", "col"), P("row", "col"))
    return jax.shard_map(shards, mesh=mesh, in_specs=in_specs, out_specs=out_specs, check_vma=False)
```

```python
import math

import jax
import jax.numpy as jnp
from jax import lax
from jax.sharding import PartitionSpec as P

TURB = 16
SPT = 512
INF = 128
NUP = 4
NAZ = 72


def broadcast(value, axis, root):
    mine = lax.axis_index(axis) == root
    return lax.psum(jnp.where(mine, value, jnp.zeros_like(value)), axis)


def observe_columns(sensor_weight, sensor_turbine, azimuth_index, start, count):
    sensors = sensor_weight.shape[0]
    matches = sensor_turbine[:, None] == jnp.arange(TURB)[None, :]
    rotor_index = jnp.sum(jnp.where(matches, azimuth_index[None, :], 0), axis=1)
    sensor_index = jnp.arange(sensors)
    blade_angle = rotor_index.astype(jnp.float32) * jnp.float32(2.0 * math.pi / NAZ) + (
        sensor_index % 3
    ).astype(jnp.float32) * jnp.float32(2.0 * math.pi / 3.0)
    positions = start + jnp.arange(count)
    turbine_of = positions // SPT
    offset_of = positions % SPT
    widened = jnp.tile(sensor_weight, (1, max(1, count // SPT)))
    weights = lax.dynamic_slice_in_dim(widened, start % SPT, count, 1)
    cosine = jnp.cos(blade_angle)[:, None]
    sine = jnp.sin(blade_angle)[:, None]
    factor = jnp.where(
        offset_of[None, :] < 2 * INF,
        jnp.float32(1.0),
        jnp.where(offset_of[None, :] < 3 * INF, cosine, sine),
    )
    return jnp.where(
        sensor_turbine[:, None] == turbine_of[None, :], weights * factor, jnp.float32(0.0)
    )


def split_bf16(x):
    high = lax.reduce_precision(x, exponent_bits=8, mantissa_bits=7)
    return high.astype(jnp.bfloat16), (x - high).astype(jnp.bfloat16)


def column_rows(local_rows, col_count):
    nrow = lax.axis_size("row")
    ncol = lax.axis_size("col")
    devices = nrow * ncol
    pieces = []
    for step in range(nrow):
        perm = [(d, ((d % nrow + step) % nrow) * ncol + d // nrow) for d in range(devices)]
        pieces.append(lax.ppermute(local_rows, ("row", "col"), perm))
    stacked = jnp.stack(pieces, 0)
    order = (lax.axis_index("row") - jnp.arange(nrow)) % nrow
    return jnp.take(stacked, order, axis=0).reshape((col_count,) + local_rows.shape[1:])


def coupling_matrix(wake_block, upstream, turbine):
    slots = upstream[turbine]
    blocks = jnp.zeros((INF, TURB, INF), jnp.bfloat16)
    for slot_index in range(NUP):
        anchor = slots[slot_index]
        hit = (jnp.arange(TURB) == anchor)[None, :, None]
        blocks = blocks + jnp.where(
            hit, wake_block[turbine, slot_index][:, None, :], jnp.zeros((), jnp.bfloat16)
        )
    return blocks.reshape(INF, TURB * INF)


def dot_f32(a, b, dims):
    return lax.dot_general(a, b, (dims, ((), ())), preferred_element_type=jnp.float32)


def shards(
    covariance,
    self_block,
    wake_block,
    upstream,
    process_noise,
    sensor_turbine,
    azimuth_index,
    sensor_weight,
    sensor_noise,
):
    row_count, col_count = covariance.shape
    row_start = lax.axis_index("row") * row_count
    col_start = lax.axis_index("col") * col_count
    per_row = row_count // SPT
    per_col = max(1, col_count // SPT)
    first_turbine = lax.axis_index("row") * per_row

    cov3 = covariance.reshape(per_row, SPT, col_count)
    inflow_part = cov3[:, :INF, :].astype(jnp.bfloat16)
    inflow_all = lax.all_gather(inflow_part, "row", axis=0, tiled=True)
    inflow_all = inflow_all.reshape(TURB * INF, col_count)
    own_rows = lax.all_gather(self_block, "col", axis=0, tiled=True)
    cov_high, cov_low = split_bf16(cov3)
    blocks = []
    for local in range(per_row):
        turbine = first_turbine + local
        diag_rows = own_rows[local * SPT : (local + 1) * SPT]
        result = dot_f32(diag_rows, cov_high[local], ((1,), (0,))) + dot_f32(
            diag_rows, cov_low[local], ((1,), (0,))
        )
        coupling = coupling_matrix(wake_block, upstream, turbine)
        inflow_sum = dot_f32(coupling, inflow_all, ((1,), (0,)))
        result = jnp.concatenate([result[:INF] + inflow_sum, result[INF:]], 0)
        blocks.append(result.astype(jnp.bfloat16))
    half_product = jnp.concatenate(blocks, 0)

    if col_count >= SPT:
        half3 = half_product.reshape(row_count, per_col, SPT)
        half_inflow = jnp.transpose(half3[:, :, :INF], (1, 0, 2))
        half_inflow_all = lax.all_gather(half_inflow, "col", axis=0, tiled=True)
        turbine_cols = [half3[:, local, :] for local in range(per_col)]
    else:
        full = lax.all_gather(half_product, "col", axis=1, tiled=True)
        half_inflow_all = jnp.transpose(full.reshape(row_count, TURB, SPT)[:, :, :INF], (1, 0, 2))
        turbine_cols = [lax.dynamic_slice_in_dim(full, (col_start // SPT) * SPT, SPT, 1)]
    target_rows = column_rows(self_block, col_count)
    piece_width = min(col_count, SPT)
    pieces = []
    for local in range(per_col):
        turbine = col_start // SPT + local
        diag_rows = target_rows[local * piece_width : (local + 1) * piece_width]
        result = dot_f32(turbine_cols[local], diag_rows, ((1,), (1,)))
        coupling = coupling_matrix(wake_block, upstream, turbine).reshape(INF, TURB, INF)
        inflow_sum = dot_f32(half_inflow_all, coupling, ((0, 2), (1, 2)))
        inflow_sum = jnp.where(col_start % SPT == 0, inflow_sum, jnp.float32(0.0))
        pieces.append(jnp.concatenate([result[:, :INF] + inflow_sum, result[:, INF:]], 1))
    predicted = jnp.concatenate(pieces, 1)
    row_ids = row_start + jnp.arange(row_count)
    col_ids = col_start + jnp.arange(col_count)
    predicted = predicted + jnp.where(
        row_ids[:, None] == col_ids[None, :], process_noise[None, :], jnp.float32(0.0)
    )

    col_observe = observe_columns(
        sensor_weight, sensor_turbine, azimuth_index, col_start, col_count
    )
    partial_cross = jnp.dot(predicted, col_observe.T, precision=lax.Precision.HIGHEST)
    cross_cov = lax.psum(partial_cross, "col")
    row_observe = observe_columns(
        sensor_weight, sensor_turbine, azimuth_index, row_start, row_count
    )
    partial_innovation = jnp.dot(row_observe, cross_cov, precision=lax.Precision.HIGHEST)
    innovation = lax.psum(partial_innovation, "row") + jnp.diag(sensor_noise)
    symmetric = 0.5 * (innovation + innovation.T)
    lower = jnp.linalg.cholesky(symmetric)
    sensors = symmetric.shape[0]
    lower_inverse = jax.scipy.linalg.solve_triangular(
        lower, jnp.eye(sensors, dtype=jnp.float32), lower=True
    )
    inverse = jnp.dot(lower_inverse.T, lower_inverse, precision=lax.Precision.HIGHEST)
    gain_block = jnp.dot(cross_cov, inverse, precision=lax.Precision.HIGHEST)
    piece = self_block.shape[0]
    own_piece = lax.dynamic_slice_in_dim(cross_cov, lax.axis_index("col") * piece, piece, 0)
    target_cross = column_rows(own_piece, col_count)
    posterior = predicted - jnp.dot(gain_block, target_cross.T, precision=lax.Precision.HIGHEST)
    share = gain_block.shape[1] // lax.axis_size("col")
    gain_share = lax.dynamic_slice_in_dim(gain_block, lax.axis_index("col") * share, share, 1)
    return (posterior, gain_share)


def solution(mesh):
    in_specs = (P("row", "col"), P(("row", "col"), None), P(), P(), P("col"), P(), P(), P(), P())
    out_specs = (P("row", "col"), P("row", "col"))
    return jax.shard_map(shards, mesh=mesh, in_specs=in_specs, out_specs=out_specs, check_vma=False)
```

```python
import math

import jax
import jax.numpy as jnp
from jax import lax
from jax.sharding import PartitionSpec as P

TURB = 16
SPT = 512
INF = 128
NUP = 4
NAZ = 72


def broadcast(value, axis, root):
    mine = lax.axis_index(axis) == root
    return lax.psum(jnp.where(mine, value, jnp.zeros_like(value)), axis)


def observe_columns(sensor_weight, sensor_turbine, azimuth_index, start, count):
    sensors = sensor_weight.shape[0]
    matches = sensor_turbine[:, None] == jnp.arange(TURB)[None, :]
    rotor_index = jnp.sum(jnp.where(matches, azimuth_index[None, :], 0), axis=1)
    sensor_index = jnp.arange(sensors)
    blade_angle = rotor_index.astype(jnp.float32) * jnp.float32(2.0 * math.pi / NAZ) + (
        sensor_index % 3
    ).astype(jnp.float32) * jnp.float32(2.0 * math.pi / 3.0)
    positions = start + jnp.arange(count)
    turbine_of = positions // SPT
    offset_of = positions % SPT
    widened = jnp.tile(sensor_weight, (1, max(1, count // SPT)))
    weights = lax.dynamic_slice_in_dim(widened, start % SPT, count, 1)
    cosine = jnp.cos(blade_angle)[:, None]
    sine = jnp.sin(blade_angle)[:, None]
    factor = jnp.where(
        offset_of[None, :] < 2 * INF,
        jnp.float32(1.0),
        jnp.where(offset_of[None, :] < 3 * INF, cosine, sine),
    )
    return jnp.where(
        sensor_turbine[:, None] == turbine_of[None, :], weights * factor, jnp.float32(0.0)
    )


def gather_col(local_rows):
    ncol = lax.axis_size("col")
    if ncol > 8:
        return lax.all_gather(local_rows, "col", axis=0, tiled=True)
    pieces = [local_rows]
    for step in range(1, ncol):
        perm = [(c, (c + step) % ncol) for c in range(ncol)]
        pieces.append(lax.ppermute(local_rows, "col", perm))
    stacked = jnp.stack(pieces, 0)
    order = (lax.axis_index("col") - jnp.arange(ncol)) % ncol
    return jnp.take(stacked, order, axis=0).reshape((-1,) + local_rows.shape[1:])


def split_bf16(x):
    high = lax.reduce_precision(x, exponent_bits=8, mantissa_bits=7)
    return high.astype(jnp.bfloat16), (x - high).astype(jnp.bfloat16)


def column_rows(local_rows, col_count):
    nrow = lax.axis_size("row")
    ncol = lax.axis_size("col")
    devices = nrow * ncol
    pieces = []
    for step in range(nrow):
        perm = [(d, ((d % nrow + step) % nrow) * ncol + d // nrow) for d in range(devices)]
        pieces.append(lax.ppermute(local_rows, ("row", "col"), perm))
    stacked = jnp.stack(pieces, 0)
    order = (lax.axis_index("row") - jnp.arange(nrow)) % nrow
    return jnp.take(stacked, order, axis=0).reshape((col_count,) + local_rows.shape[1:])


def coupling_matrix(wake_block, upstream, turbine):
    slots = upstream[turbine]
    blocks = jnp.zeros((INF, TURB, INF), jnp.bfloat16)
    for slot_index in range(NUP):
        anchor = slots[slot_index]
        hit = (jnp.arange(TURB) == anchor)[None, :, None]
        blocks = blocks + jnp.where(
            hit, wake_block[turbine, slot_index][:, None, :], jnp.zeros((), jnp.bfloat16)
        )
    return blocks.reshape(INF, TURB * INF)


def dot_f32(a, b, dims):
    return lax.dot_general(a, b, (dims, ((), ())), preferred_element_type=jnp.float32)


def shards(
    covariance,
    self_block,
    wake_block,
    upstream,
    process_noise,
    sensor_turbine,
    azimuth_index,
    sensor_weight,
    sensor_noise,
):
    row_count, col_count = covariance.shape
    row_start = lax.axis_index("row") * row_count
    col_start = lax.axis_index("col") * col_count
    per_row = row_count // SPT
    per_col = max(1, col_count // SPT)
    first_turbine = lax.axis_index("row") * per_row

    cov3 = covariance.reshape(per_row, SPT, col_count)
    inflow_part = cov3[:, :INF, :].astype(jnp.bfloat16)
    inflow_all = lax.all_gather(inflow_part, "row", axis=0, tiled=True)
    inflow_all = inflow_all.reshape(TURB * INF, col_count)
    own_rows = gather_col(self_block)
    cov_high, cov_low = split_bf16(cov3)
    blocks = []
    for local in range(per_row):
        turbine = first_turbine + local
        diag_rows = own_rows[local * SPT : (local + 1) * SPT]
        result = dot_f32(diag_rows, cov_high[local], ((1,), (0,))) + dot_f32(
            diag_rows, cov_low[local], ((1,), (0,))
        )
        coupling = coupling_matrix(wake_block, upstream, turbine)
        inflow_sum = dot_f32(coupling, inflow_all, ((1,), (0,)))
        result = jnp.concatenate([result[:INF] + inflow_sum, result[INF:]], 0)
        blocks.append(result.astype(jnp.bfloat16))
    half_product = jnp.concatenate(blocks, 0)

    if col_count >= SPT:
        half3 = half_product.reshape(row_count, per_col, SPT)
        half_inflow = jnp.transpose(half3[:, :, :INF], (1, 0, 2))
        half_inflow_all = lax.all_gather(half_inflow, "col", axis=0, tiled=True)
        turbine_cols = [half3[:, local, :] for local in range(per_col)]
    else:
        full = lax.all_gather(half_product, "col", axis=1, tiled=True)
        half_inflow_all = jnp.transpose(full.reshape(row_count, TURB, SPT)[:, :, :INF], (1, 0, 2))
        turbine_cols = [lax.dynamic_slice_in_dim(full, (col_start // SPT) * SPT, SPT, 1)]
    target_rows = column_rows(self_block, col_count)
    piece_width = min(col_count, SPT)
    pieces = []
    for local in range(per_col):
        turbine = col_start // SPT + local
        diag_rows = target_rows[local * piece_width : (local + 1) * piece_width]
        result = dot_f32(turbine_cols[local], diag_rows, ((1,), (1,)))
        coupling = coupling_matrix(wake_block, upstream, turbine).reshape(INF, TURB, INF)
        inflow_sum = dot_f32(half_inflow_all, coupling, ((0, 2), (1, 2)))
        inflow_sum = jnp.where(col_start % SPT == 0, inflow_sum, jnp.float32(0.0))
        pieces.append(jnp.concatenate([result[:, :INF] + inflow_sum, result[:, INF:]], 1))
    predicted = jnp.concatenate(pieces, 1)
    row_ids = row_start + jnp.arange(row_count)
    col_ids = col_start + jnp.arange(col_count)
    predicted = predicted + jnp.where(
        row_ids[:, None] == col_ids[None, :], process_noise[None, :], jnp.float32(0.0)
    )

    col_observe = observe_columns(
        sensor_weight, sensor_turbine, azimuth_index, col_start, col_count
    )
    partial_cross = jnp.dot(predicted, col_observe.T, precision=lax.Precision.HIGHEST)
    row_observe = observe_columns(
        sensor_weight, sensor_turbine, azimuth_index, row_start, row_count
    )
    partial_innovation = jnp.dot(row_observe, partial_cross, precision=lax.Precision.HIGHEST)
    innovation = lax.psum(partial_innovation, ("row", "col")) + jnp.diag(sensor_noise)
    partial_cross, innovation = lax.optimization_barrier((partial_cross, innovation))
    cross_cov = lax.psum(partial_cross, "col")
    symmetric = 0.5 * (innovation + innovation.T)
    lower = jnp.linalg.cholesky(symmetric)
    sensors = symmetric.shape[0]
    lower_inverse = jax.scipy.linalg.solve_triangular(
        lower, jnp.eye(sensors, dtype=jnp.float32), lower=True
    )
    inverse = jnp.dot(lower_inverse.T, lower_inverse, precision=lax.Precision.HIGHEST)
    gain_block = jnp.dot(cross_cov, inverse, precision=lax.Precision.HIGHEST)
    piece = self_block.shape[0]
    own_piece = lax.dynamic_slice_in_dim(cross_cov, lax.axis_index("col") * piece, piece, 0)
    target_cross = column_rows(own_piece, col_count)
    posterior = predicted - jnp.dot(gain_block, target_cross.T, precision=lax.Precision.HIGHEST)
    share = gain_block.shape[1] // lax.axis_size("col")
    gain_share = lax.dynamic_slice_in_dim(gain_block, lax.axis_index("col") * share, share, 1)
    return (posterior, gain_share)


def solution(mesh):
    in_specs = (P("row", "col"), P(("row", "col"), None), P(), P(), P("col"), P(), P(), P(), P())
    out_specs = (P("row", "col"), P("row", "col"))
    return jax.shard_map(shards, mesh=mesh, in_specs=in_specs, out_specs=out_specs, check_vma=False)
```

```python
import math

import jax
import jax.numpy as jnp
from jax import lax
from jax.sharding import PartitionSpec as P

TURB = 16
SPT = 512
INF = 128
NUP = 4
NAZ = 72


def broadcast(value, axis, root):
    mine = lax.axis_index(axis) == root
    return lax.psum(jnp.where(mine, value, jnp.zeros_like(value)), axis)


def observe_columns(sensor_weight, sensor_turbine, azimuth_index, start, count):
    sensors = sensor_weight.shape[0]
    matches = sensor_turbine[:, None] == jnp.arange(TURB)[None, :]
    rotor_index = jnp.sum(jnp.where(matches, azimuth_index[None, :], 0), axis=1)
    sensor_index = jnp.arange(sensors)
    blade_angle = rotor_index.astype(jnp.float32) * jnp.float32(2.0 * math.pi / NAZ) + (
        sensor_index % 3
    ).astype(jnp.float32) * jnp.float32(2.0 * math.pi / 3.0)
    positions = start + jnp.arange(count)
    turbine_of = positions // SPT
    offset_of = positions % SPT
    widened = jnp.tile(sensor_weight, (1, max(1, count // SPT)))
    weights = lax.dynamic_slice_in_dim(widened, start % SPT, count, 1)
    cosine = jnp.cos(blade_angle)[:, None]
    sine = jnp.sin(blade_angle)[:, None]
    factor = jnp.where(
        offset_of[None, :] < 2 * INF,
        jnp.float32(1.0),
        jnp.where(offset_of[None, :] < 3 * INF, cosine, sine),
    )
    return jnp.where(
        sensor_turbine[:, None] == turbine_of[None, :], weights * factor, jnp.float32(0.0)
    )


def gather_col(local_rows):
    ncol = lax.axis_size("col")
    if ncol > 8:
        return lax.all_gather(local_rows, "col", axis=0, tiled=True)
    pieces = [local_rows]
    for step in range(1, ncol):
        perm = [(c, (c + step) % ncol) for c in range(ncol)]
        pieces.append(lax.ppermute(local_rows, "col", perm))
    stacked = jnp.stack(pieces, 0)
    order = (lax.axis_index("col") - jnp.arange(ncol)) % ncol
    return jnp.take(stacked, order, axis=0).reshape((-1,) + local_rows.shape[1:])


def split_bf16(x):
    high = lax.reduce_precision(x, exponent_bits=8, mantissa_bits=7)
    return high.astype(jnp.bfloat16), (x - high).astype(jnp.bfloat16)


def column_rows(local_rows, col_count):
    nrow = lax.axis_size("row")
    ncol = lax.axis_size("col")
    devices = nrow * ncol
    pieces = []
    for step in range(nrow):
        perm = [(d, ((d % nrow + step) % nrow) * ncol + d // nrow) for d in range(devices)]
        pieces.append(lax.ppermute(local_rows, ("row", "col"), perm))
    stacked = jnp.stack(pieces, 0)
    order = (lax.axis_index("row") - jnp.arange(nrow)) % nrow
    return jnp.take(stacked, order, axis=0).reshape((col_count,) + local_rows.shape[1:])


def coupling_matrix(wake_block, upstream, turbine):
    slots = upstream[turbine]
    blocks = jnp.zeros((INF, TURB, INF), jnp.bfloat16)
    for slot_index in range(NUP):
        anchor = slots[slot_index]
        hit = (jnp.arange(TURB) == anchor)[None, :, None]
        blocks = blocks + jnp.where(
            hit, wake_block[turbine, slot_index][:, None, :], jnp.zeros((), jnp.bfloat16)
        )
    return blocks.reshape(INF, TURB * INF)


def mm(a, b):
    return jnp.dot(a, b, precision=lax.Precision.HIGHEST)


def cholesky_inverse(symmetric):
    size = symmetric.shape[0]
    block = 128 if size % 128 == 0 else size
    count = size // block
    eye = jnp.eye(block, dtype=jnp.float32)
    work = {
        (i, j): symmetric[i * block : (i + 1) * block, j * block : (j + 1) * block]
        for i in range(count)
        for j in range(i + 1)
    }
    lower = {}
    diag_inverse = {}
    for k in range(count):
        lower[k, k] = jnp.linalg.cholesky(work[k, k])
        diag_inverse[k] = jax.scipy.linalg.solve_triangular(lower[k, k], eye, lower=True)
        for i in range(k + 1, count):
            lower[i, k] = mm(work[i, k], diag_inverse[k].T)
        for i in range(k + 1, count):
            for j in range(k + 1, i + 1):
                work[i, j] = work[i, j] - mm(lower[i, k], lower[j, k].T)
    inv = {}
    for i in range(count):
        inv[i, i] = diag_inverse[i]
        for j in range(i - 1, -1, -1):
            total = sum(mm(lower[i, m], inv[m, j]) for m in range(j, i))
            inv[i, j] = -mm(diag_inverse[i], total)
    zero = jnp.zeros((block, block), jnp.float32)
    lower_inverse = jnp.block(
        [[inv[i, j] if j <= i else zero for j in range(count)] for i in range(count)]
    )
    return mm(lower_inverse.T, lower_inverse)


def dot_f32(a, b, dims):
    return lax.dot_general(a, b, (dims, ((), ())), preferred_element_type=jnp.float32)


def shards(
    covariance,
    self_block,
    wake_block,
    upstream,
    process_noise,
    sensor_turbine,
    azimuth_index,
    sensor_weight,
    sensor_noise,
):
    row_count, col_count = covariance.shape
    row_start = lax.axis_index("row") * row_count
    col_start = lax.axis_index("col") * col_count
    per_row = row_count // SPT
    per_col = max(1, col_count // SPT)
    first_turbine = lax.axis_index("row") * per_row

    cov3 = covariance.reshape(per_row, SPT, col_count)
    inflow_part = cov3[:, :INF, :].astype(jnp.bfloat16)
    inflow_all = lax.all_gather(inflow_part, "row", axis=0, tiled=True)
    inflow_all = inflow_all.reshape(TURB * INF, col_count)
    own_rows = gather_col(self_block)
    cov_high, cov_low = split_bf16(cov3)
    blocks = []
    for local in range(per_row):
        turbine = first_turbine + local
        diag_rows = own_rows[local * SPT : (local + 1) * SPT]
        result = dot_f32(diag_rows, cov_high[local], ((1,), (0,))) + dot_f32(
            diag_rows, cov_low[local], ((1,), (0,))
        )
        coupling = coupling_matrix(wake_block, upstream, turbine)
        inflow_sum = dot_f32(coupling, inflow_all, ((1,), (0,)))
        result = jnp.concatenate([result[:INF] + inflow_sum, result[INF:]], 0)
        blocks.append(result.astype(jnp.bfloat16))
    half_product = jnp.concatenate(blocks, 0)

    if col_count >= SPT:
        half3 = half_product.reshape(row_count, per_col, SPT)
        half_inflow = jnp.transpose(half3[:, :, :INF], (1, 0, 2))
        half_inflow_all = lax.all_gather(half_inflow, "col", axis=0, tiled=True)
        turbine_cols = [half3[:, local, :] for local in range(per_col)]
    else:
        full = lax.all_gather(half_product, "col", axis=1, tiled=True)
        half_inflow_all = jnp.transpose(full.reshape(row_count, TURB, SPT)[:, :, :INF], (1, 0, 2))
        turbine_cols = [lax.dynamic_slice_in_dim(full, (col_start // SPT) * SPT, SPT, 1)]
    target_rows = column_rows(self_block, col_count)
    piece_width = min(col_count, SPT)
    pieces = []
    for local in range(per_col):
        turbine = col_start // SPT + local
        diag_rows = target_rows[local * piece_width : (local + 1) * piece_width]
        result = dot_f32(turbine_cols[local], diag_rows, ((1,), (1,)))
        coupling = coupling_matrix(wake_block, upstream, turbine).reshape(INF, TURB, INF)
        inflow_sum = dot_f32(half_inflow_all, coupling, ((0, 2), (1, 2)))
        inflow_sum = jnp.where(col_start % SPT == 0, inflow_sum, jnp.float32(0.0))
        pieces.append(jnp.concatenate([result[:, :INF] + inflow_sum, result[:, INF:]], 1))
    predicted = jnp.concatenate(pieces, 1)
    row_ids = row_start + jnp.arange(row_count)
    col_ids = col_start + jnp.arange(col_count)
    predicted = predicted + jnp.where(
        row_ids[:, None] == col_ids[None, :], process_noise[None, :], jnp.float32(0.0)
    )

    col_observe = observe_columns(
        sensor_weight, sensor_turbine, azimuth_index, col_start, col_count
    )
    partial_cross = jnp.dot(predicted, col_observe.T, precision=lax.Precision.HIGHEST)
    cross_cov = lax.psum(partial_cross, "col")
    row_observe = observe_columns(
        sensor_weight, sensor_turbine, azimuth_index, row_start, row_count
    )
    partial_innovation = jnp.dot(row_observe, cross_cov, precision=lax.Precision.HIGHEST)
    innovation = lax.psum(partial_innovation, "row") + jnp.diag(sensor_noise)
    symmetric = 0.5 * (innovation + innovation.T)
    inverse = cholesky_inverse(symmetric)
    gain_block = jnp.dot(cross_cov, inverse, precision=lax.Precision.HIGHEST)
    piece = self_block.shape[0]
    own_piece = lax.dynamic_slice_in_dim(cross_cov, lax.axis_index("col") * piece, piece, 0)
    target_cross = column_rows(own_piece, col_count)
    posterior = predicted - jnp.dot(gain_block, target_cross.T, precision=lax.Precision.HIGHEST)
    share = gain_block.shape[1] // lax.axis_size("col")
    gain_share = lax.dynamic_slice_in_dim(gain_block, lax.axis_index("col") * share, share, 1)
    return (posterior, gain_share)


def solution(mesh):
    in_specs = (P("row", "col"), P(("row", "col"), None), P(), P(), P("col"), P(), P(), P(), P())
    out_specs = (P("row", "col"), P("row", "col"))
    return jax.shard_map(shards, mesh=mesh, in_specs=in_specs, out_specs=out_specs, check_vma=False)
```

```python
import math

import jax
import jax.numpy as jnp
from jax import lax
from jax.sharding import PartitionSpec as P

TURB = 16
SPT = 512
INF = 128
NUP = 4
NAZ = 72


def broadcast(value, axis, root):
    mine = lax.axis_index(axis) == root
    return lax.psum(jnp.where(mine, value, jnp.zeros_like(value)), axis)


def observe_columns(sensor_weight, sensor_turbine, azimuth_index, start, count):
    sensors = sensor_weight.shape[0]
    matches = sensor_turbine[:, None] == jnp.arange(TURB)[None, :]
    rotor_index = jnp.sum(jnp.where(matches, azimuth_index[None, :], 0), axis=1)
    sensor_index = jnp.arange(sensors)
    blade_angle = rotor_index.astype(jnp.float32) * jnp.float32(2.0 * math.pi / NAZ) + (
        sensor_index % 3
    ).astype(jnp.float32) * jnp.float32(2.0 * math.pi / 3.0)
    positions = start + jnp.arange(count)
    turbine_of = positions // SPT
    offset_of = positions % SPT
    widened = jnp.tile(sensor_weight, (1, max(1, count // SPT)))
    weights = lax.dynamic_slice_in_dim(widened, start % SPT, count, 1)
    cosine = jnp.cos(blade_angle)[:, None]
    sine = jnp.sin(blade_angle)[:, None]
    factor = jnp.where(
        offset_of[None, :] < 2 * INF,
        jnp.float32(1.0),
        jnp.where(offset_of[None, :] < 3 * INF, cosine, sine),
    )
    return jnp.where(
        sensor_turbine[:, None] == turbine_of[None, :], weights * factor, jnp.float32(0.0)
    )


def gather_col(local_rows):
    ncol = lax.axis_size("col")
    if ncol > 8:
        return lax.all_gather(local_rows, "col", axis=0, tiled=True)
    pieces = [local_rows]
    for step in range(1, ncol):
        perm = [(c, (c + step) % ncol) for c in range(ncol)]
        pieces.append(lax.ppermute(local_rows, "col", perm))
    stacked = jnp.stack(pieces, 0)
    order = (lax.axis_index("col") - jnp.arange(ncol)) % ncol
    return jnp.take(stacked, order, axis=0).reshape((-1,) + local_rows.shape[1:])


def split_bf16(x):
    high = lax.reduce_precision(x, exponent_bits=8, mantissa_bits=7)
    return high.astype(jnp.bfloat16), (x - high).astype(jnp.bfloat16)


def column_rows(local_rows, col_count):
    nrow = lax.axis_size("row")
    ncol = lax.axis_size("col")
    devices = nrow * ncol
    pieces = []
    for step in range(nrow):
        perm = [(d, ((d % nrow + step) % nrow) * ncol + d // nrow) for d in range(devices)]
        pieces.append(lax.ppermute(local_rows, ("row", "col"), perm))
    stacked = jnp.stack(pieces, 0)
    order = (lax.axis_index("row") - jnp.arange(nrow)) % nrow
    return jnp.take(stacked, order, axis=0).reshape((col_count,) + local_rows.shape[1:])


def coupling_matrix(wake_block, upstream, turbine):
    slots = upstream[turbine]
    blocks = jnp.zeros((INF, TURB, INF), jnp.bfloat16)
    for slot_index in range(NUP):
        anchor = slots[slot_index]
        hit = (jnp.arange(TURB) == anchor)[None, :, None]
        blocks = blocks + jnp.where(
            hit, wake_block[turbine, slot_index][:, None, :], jnp.zeros((), jnp.bfloat16)
        )
    return blocks.reshape(INF, TURB * INF)


def mm(a, b):
    return jnp.dot(a, b, precision=lax.Precision.HIGHEST)


def cholesky_inverse(symmetric):
    size = symmetric.shape[0]
    block = 128 if size % 128 == 0 else size
    count = size // block
    eye = jnp.eye(block, dtype=jnp.float32)
    work = {
        (i, j): symmetric[i * block : (i + 1) * block, j * block : (j + 1) * block]
        for i in range(count)
        for j in range(i + 1)
    }
    lower = {}
    diag_inverse = {}
    for k in range(count):
        lower[k, k] = jnp.linalg.cholesky(work[k, k])
        diag_inverse[k] = jax.scipy.linalg.solve_triangular(lower[k, k], eye, lower=True)
        for i in range(k + 1, count):
            lower[i, k] = mm(work[i, k], diag_inverse[k].T)
        for i in range(k + 1, count):
            for j in range(k + 1, i + 1):
                work[i, j] = work[i, j] - mm(lower[i, k], lower[j, k].T)
    inv = {}
    for i in range(count):
        inv[i, i] = diag_inverse[i]
        for j in range(i - 1, -1, -1):
            total = sum(mm(lower[i, m], inv[m, j]) for m in range(j, i))
            inv[i, j] = -mm(diag_inverse[i], total)
    zero = jnp.zeros((block, block), jnp.float32)
    lower_inverse = jnp.block(
        [[inv[i, j] if j <= i else zero for j in range(count)] for i in range(count)]
    )
    return mm(lower_inverse.T, lower_inverse)


def dot_f32(a, b, dims):
    return lax.dot_general(a, b, (dims, ((), ())), preferred_element_type=jnp.float32)


def shards(
    covariance,
    self_block,
    wake_block,
    upstream,
    process_noise,
    sensor_turbine,
    azimuth_index,
    sensor_weight,
    sensor_noise,
):
    row_count, col_count = covariance.shape
    row_start = lax.axis_index("row") * row_count
    col_start = lax.axis_index("col") * col_count
    per_row = row_count // SPT
    per_col = max(1, col_count // SPT)
    first_turbine = lax.axis_index("row") * per_row

    cov3 = covariance.reshape(per_row, SPT, col_count)
    inflow_part = cov3[:, :INF, :].astype(jnp.bfloat16)
    inflow_all = lax.all_gather(inflow_part, "row", axis=0, tiled=True)
    inflow_all = inflow_all.reshape(TURB * INF, col_count)
    own_rows = gather_col(self_block)
    cov_high, cov_low = split_bf16(cov3)
    blocks = []
    for local in range(per_row):
        turbine = first_turbine + local
        diag_rows = own_rows[local * SPT : (local + 1) * SPT]
        result = dot_f32(diag_rows, cov_high[local], ((1,), (0,))) + dot_f32(
            diag_rows, cov_low[local], ((1,), (0,))
        )
        coupling = coupling_matrix(wake_block, upstream, turbine)
        inflow_sum = dot_f32(coupling, inflow_all, ((1,), (0,)))
        result = jnp.concatenate([result[:INF] + inflow_sum, result[INF:]], 0)
        blocks.append(result.astype(jnp.bfloat16))
    half_product = jnp.concatenate(blocks, 0)

    if col_count >= SPT:
        half3 = half_product.reshape(row_count, per_col, SPT)
        half_inflow = jnp.transpose(half3[:, :, :INF], (1, 0, 2))
        half_inflow_all = lax.all_gather(half_inflow, "col", axis=0, tiled=True)
        turbine_cols = [half3[:, local, :] for local in range(per_col)]
    else:
        full = lax.all_gather(half_product, "col", axis=1, tiled=True)
        half_inflow_all = jnp.transpose(full.reshape(row_count, TURB, SPT)[:, :, :INF], (1, 0, 2))
        turbine_cols = [lax.dynamic_slice_in_dim(full, (col_start // SPT) * SPT, SPT, 1)]
    target_rows = column_rows(self_block, col_count)
    piece_width = min(col_count, SPT)
    pieces = []
    for local in range(per_col):
        turbine = col_start // SPT + local
        diag_rows = target_rows[local * piece_width : (local + 1) * piece_width]
        result = lax.optimization_barrier(dot_f32(turbine_cols[local], diag_rows, ((1,), (1,))))
        coupling = coupling_matrix(wake_block, upstream, turbine).reshape(INF, TURB, INF)
        inflow_sum = dot_f32(half_inflow_all, coupling, ((0, 2), (1, 2)))
        inflow_sum = jnp.where(col_start % SPT == 0, inflow_sum, jnp.float32(0.0))
        pieces.append(jnp.concatenate([result[:, :INF] + inflow_sum, result[:, INF:]], 1))
    predicted = jnp.concatenate(pieces, 1)
    row_ids = row_start + jnp.arange(row_count)
    col_ids = col_start + jnp.arange(col_count)
    predicted = predicted + jnp.where(
        row_ids[:, None] == col_ids[None, :], process_noise[None, :], jnp.float32(0.0)
    )
    predicted = lax.optimization_barrier(predicted)

    col_observe = observe_columns(
        sensor_weight, sensor_turbine, azimuth_index, col_start, col_count
    )
    partial_cross = jnp.dot(predicted, col_observe.T, precision=lax.Precision.HIGH)
    cross_cov = lax.psum(partial_cross, "col")
    row_observe = observe_columns(
        sensor_weight, sensor_turbine, azimuth_index, row_start, row_count
    )
    partial_innovation = jnp.dot(row_observe, cross_cov, precision=lax.Precision.HIGHEST)
    innovation = lax.psum(partial_innovation, "row") + jnp.diag(sensor_noise)
    symmetric = 0.5 * (innovation + innovation.T)
    inverse = cholesky_inverse(symmetric)
    gain_block = jnp.dot(cross_cov, inverse, precision=lax.Precision.HIGH)
    piece = self_block.shape[0]
    own_piece = lax.dynamic_slice_in_dim(cross_cov, lax.axis_index("col") * piece, piece, 0)
    own_piece, innovation = lax.optimization_barrier((own_piece, innovation))
    target_cross = column_rows(own_piece, col_count)
    posterior = predicted - jnp.dot(gain_block, target_cross.T, precision=lax.Precision.HIGH)
    share = gain_block.shape[1] // lax.axis_size("col")
    gain_share = lax.dynamic_slice_in_dim(gain_block, lax.axis_index("col") * share, share, 1)
    return (posterior, gain_share)


def solution(mesh):
    in_specs = (P("row", "col"), P(("row", "col"), None), P(), P(), P("col"), P(), P(), P(), P())
    out_specs = (P("row", "col"), P("row", "col"))
    return jax.shard_map(shards, mesh=mesh, in_specs=in_specs, out_specs=out_specs, check_vma=False)
```

```python
import math

import jax
import jax.numpy as jnp
from jax import lax
from jax.sharding import PartitionSpec as P

TURB = 16
SPT = 512
INF = 128
NUP = 4
NAZ = 72


def broadcast(value, axis, root):
    mine = lax.axis_index(axis) == root
    return lax.psum(jnp.where(mine, value, jnp.zeros_like(value)), axis)


def observe_columns(sensor_weight, sensor_turbine, azimuth_index, start, count):
    sensors = sensor_weight.shape[0]
    matches = sensor_turbine[:, None] == jnp.arange(TURB)[None, :]
    rotor_index = jnp.sum(jnp.where(matches, azimuth_index[None, :], 0), axis=1)
    sensor_index = jnp.arange(sensors)
    blade_angle = rotor_index.astype(jnp.float32) * jnp.float32(2.0 * math.pi / NAZ) + (
        sensor_index % 3
    ).astype(jnp.float32) * jnp.float32(2.0 * math.pi / 3.0)
    positions = start + jnp.arange(count)
    turbine_of = positions // SPT
    offset_of = positions % SPT
    widened = jnp.tile(sensor_weight, (1, max(1, count // SPT)))
    weights = lax.dynamic_slice_in_dim(widened, start % SPT, count, 1)
    cosine = jnp.cos(blade_angle)[:, None]
    sine = jnp.sin(blade_angle)[:, None]
    factor = jnp.where(
        offset_of[None, :] < 2 * INF,
        jnp.float32(1.0),
        jnp.where(offset_of[None, :] < 3 * INF, cosine, sine),
    )
    return jnp.where(
        sensor_turbine[:, None] == turbine_of[None, :], weights * factor, jnp.float32(0.0)
    )


def gather_col(local_rows):
    ncol = lax.axis_size("col")
    if ncol > 8:
        return lax.all_gather(local_rows, "col", axis=0, tiled=True)
    pieces = [local_rows]
    for step in range(1, ncol):
        perm = [(c, (c + step) % ncol) for c in range(ncol)]
        pieces.append(lax.ppermute(local_rows, "col", perm))
    stacked = jnp.stack(pieces, 0)
    order = (lax.axis_index("col") - jnp.arange(ncol)) % ncol
    return jnp.take(stacked, order, axis=0).reshape((-1,) + local_rows.shape[1:])


def gather_col_paired(local):
    ncol = lax.axis_size("col")
    if ncol % 2 or ncol > 8:
        return lax.all_gather(local, "col", axis=0, tiled=True)
    col = lax.axis_index("col")
    shifts = list(range(0, ncol, 2))
    mine = [local]
    for step in shifts[1:]:
        perm = [(c, (c + step) % ncol) for c in range(ncol)]
        mine.append(lax.ppermute(local, "col", perm))
    mine = jnp.stack(mine, 0)
    theirs = lax.ppermute(mine, "col", [(c, c ^ 1) for c in range(ncol)])
    stacked = jnp.concatenate([mine, theirs], 0)
    steps = jnp.asarray(shifts, jnp.int32)
    sources = jnp.concatenate([(col - steps) % ncol, ((col ^ 1) - steps) % ncol])
    order = jnp.argsort(sources)
    return jnp.take(stacked, order, axis=0).reshape((-1,) + local.shape[1:])


def split_bf16(x):
    high = lax.reduce_precision(x, exponent_bits=8, mantissa_bits=7)
    return high.astype(jnp.bfloat16), (x - high).astype(jnp.bfloat16)


def column_rows(local_rows, col_count):
    nrow = lax.axis_size("row")
    ncol = lax.axis_size("col")
    devices = nrow * ncol
    pieces = []
    for step in range(nrow):
        perm = [(d, ((d % nrow + step) % nrow) * ncol + d // nrow) for d in range(devices)]
        pieces.append(lax.ppermute(local_rows, ("row", "col"), perm))
    stacked = jnp.stack(pieces, 0)
    order = (lax.axis_index("row") - jnp.arange(nrow)) % nrow
    return jnp.take(stacked, order, axis=0).reshape((col_count,) + local_rows.shape[1:])


def coupling_matrix(wake_block, upstream, turbine):
    slots = upstream[turbine]
    blocks = jnp.zeros((INF, TURB, INF), jnp.bfloat16)
    for slot_index in range(NUP):
        anchor = slots[slot_index]
        hit = (jnp.arange(TURB) == anchor)[None, :, None]
        blocks = blocks + jnp.where(
            hit, wake_block[turbine, slot_index][:, None, :], jnp.zeros((), jnp.bfloat16)
        )
    return blocks.reshape(INF, TURB * INF)


def mm(a, b):
    return jnp.dot(a, b, precision=lax.Precision.HIGHEST)


def cholesky_inverse(symmetric):
    size = symmetric.shape[0]
    block = 128 if size % 128 == 0 else size
    count = size // block
    eye = jnp.eye(block, dtype=jnp.float32)
    work = {
        (i, j): symmetric[i * block : (i + 1) * block, j * block : (j + 1) * block]
        for i in range(count)
        for j in range(i + 1)
    }
    lower = {}
    diag_inverse = {}
    for k in range(count):
        lower[k, k] = jnp.linalg.cholesky(work[k, k])
        diag_inverse[k] = jax.scipy.linalg.solve_triangular(lower[k, k], eye, lower=True)
        for i in range(k + 1, count):
            lower[i, k] = mm(work[i, k], diag_inverse[k].T)
        for i in range(k + 1, count):
            for j in range(k + 1, i + 1):
                work[i, j] = work[i, j] - mm(lower[i, k], lower[j, k].T)
    inv = {}
    for i in range(count):
        inv[i, i] = diag_inverse[i]
        for j in range(i - 1, -1, -1):
            total = sum(mm(lower[i, m], inv[m, j]) for m in range(j, i))
            inv[i, j] = -mm(diag_inverse[i], total)
    zero = jnp.zeros((block, block), jnp.float32)
    lower_inverse = jnp.block(
        [[inv[i, j] if j <= i else zero for j in range(count)] for i in range(count)]
    )
    return mm(lower_inverse.T, lower_inverse)


def dot_f32(a, b, dims):
    return lax.dot_general(a, b, (dims, ((), ())), preferred_element_type=jnp.float32)


def shards(
    covariance,
    self_block,
    wake_block,
    upstream,
    process_noise,
    sensor_turbine,
    azimuth_index,
    sensor_weight,
    sensor_noise,
):
    row_count, col_count = covariance.shape
    row_start = lax.axis_index("row") * row_count
    col_start = lax.axis_index("col") * col_count
    per_row = row_count // SPT
    per_col = max(1, col_count // SPT)
    first_turbine = lax.axis_index("row") * per_row

    cov3 = covariance.reshape(per_row, SPT, col_count)
    inflow_part = cov3[:, :INF, :].astype(jnp.bfloat16)
    inflow_all = lax.all_gather(inflow_part, "row", axis=0, tiled=True)
    inflow_all = inflow_all.reshape(TURB * INF, col_count)
    own_rows = gather_col(self_block)
    cov_high, cov_low = split_bf16(cov3)
    blocks = []
    for local in range(per_row):
        turbine = first_turbine + local
        diag_rows = own_rows[local * SPT : (local + 1) * SPT]
        result = dot_f32(diag_rows, cov_high[local], ((1,), (0,))) + dot_f32(
            diag_rows, cov_low[local], ((1,), (0,))
        )
        coupling = coupling_matrix(wake_block, upstream, turbine)
        inflow_sum = dot_f32(coupling, inflow_all, ((1,), (0,)))
        result = jnp.concatenate([result[:INF] + inflow_sum, result[INF:]], 0)
        blocks.append(result.astype(jnp.bfloat16))
    half_product = jnp.concatenate(blocks, 0)

    if col_count >= SPT:
        half3 = half_product.reshape(row_count, per_col, SPT)
        half_inflow = jnp.transpose(half3[:, :, :INF], (1, 0, 2))
        half_inflow_all = gather_col_paired(half_inflow)
        turbine_cols = [half3[:, local, :] for local in range(per_col)]
    else:
        full = lax.all_gather(half_product, "col", axis=1, tiled=True)
        half_inflow_all = jnp.transpose(full.reshape(row_count, TURB, SPT)[:, :, :INF], (1, 0, 2))
        turbine_cols = [lax.dynamic_slice_in_dim(full, (col_start // SPT) * SPT, SPT, 1)]
    target_rows = column_rows(self_block, col_count)
    piece_width = min(col_count, SPT)
    pieces = []
    for local in range(per_col):
        turbine = col_start // SPT + local
        diag_rows = target_rows[local * piece_width : (local + 1) * piece_width]
        result = lax.optimization_barrier(dot_f32(turbine_cols[local], diag_rows, ((1,), (1,))))
        coupling = coupling_matrix(wake_block, upstream, turbine).reshape(INF, TURB, INF)
        inflow_sum = dot_f32(half_inflow_all, coupling, ((0, 2), (1, 2)))
        inflow_sum = jnp.where(col_start % SPT == 0, inflow_sum, jnp.float32(0.0))
        pieces.append(jnp.concatenate([result[:, :INF] + inflow_sum, result[:, INF:]], 1))
    predicted = jnp.concatenate(pieces, 1)
    row_ids = row_start + jnp.arange(row_count)
    col_ids = col_start + jnp.arange(col_count)
    predicted = predicted + jnp.where(
        row_ids[:, None] == col_ids[None, :], process_noise[None, :], jnp.float32(0.0)
    )
    predicted = lax.optimization_barrier(predicted)

    col_observe = observe_columns(
        sensor_weight, sensor_turbine, azimuth_index, col_start, col_count
    )
    partial_cross = jnp.dot(predicted, col_observe.T, precision=lax.Precision.HIGH)
    cross_cov = lax.psum(partial_cross, "col")
    row_observe = observe_columns(
        sensor_weight, sensor_turbine, azimuth_index, row_start, row_count
    )
    partial_innovation = jnp.dot(row_observe, cross_cov, precision=lax.Precision.HIGH)
    innovation = lax.psum(partial_innovation, "row") + jnp.diag(sensor_noise)
    symmetric = 0.5 * (innovation + innovation.T)
    inverse = cholesky_inverse(symmetric)
    gain_block = jnp.dot(cross_cov, inverse, precision=lax.Precision.HIGH)
    piece = self_block.shape[0]
    own_piece = lax.dynamic_slice_in_dim(cross_cov, lax.axis_index("col") * piece, piece, 0)
    own_piece, innovation = lax.optimization_barrier((own_piece, innovation))
    target_cross = column_rows(own_piece, col_count)
    posterior = predicted - jnp.dot(gain_block, target_cross.T, precision=lax.Precision.HIGH)
    share = gain_block.shape[1] // lax.axis_size("col")
    gain_share = lax.dynamic_slice_in_dim(gain_block, lax.axis_index("col") * share, share, 1)
    return (posterior, gain_share)


def solution(mesh):
    in_specs = (P("row", "col"), P(("row", "col"), None), P(), P(), P("col"), P(), P(), P(), P())
    out_specs = (P("row", "col"), P("row", "col"))
    return jax.shard_map(shards, mesh=mesh, in_specs=in_specs, out_specs=out_specs, check_vma=False)
```

```python
import math

import jax
import jax.numpy as jnp
from jax import lax
from jax.sharding import PartitionSpec as P

TURB = 16
SPT = 512
INF = 128
NUP = 4
NAZ = 72


def broadcast(value, axis, root):
    mine = lax.axis_index(axis) == root
    return lax.psum(jnp.where(mine, value, jnp.zeros_like(value)), axis)


def observe_columns(sensor_weight, sensor_turbine, azimuth_index, start, count):
    sensors = sensor_weight.shape[0]
    matches = sensor_turbine[:, None] == jnp.arange(TURB)[None, :]
    rotor_index = jnp.sum(jnp.where(matches, azimuth_index[None, :], 0), axis=1)
    sensor_index = jnp.arange(sensors)
    blade_angle = rotor_index.astype(jnp.float32) * jnp.float32(2.0 * math.pi / NAZ) + (
        sensor_index % 3
    ).astype(jnp.float32) * jnp.float32(2.0 * math.pi / 3.0)
    positions = start + jnp.arange(count)
    turbine_of = positions // SPT
    offset_of = positions % SPT
    widened = jnp.tile(sensor_weight, (1, max(1, count // SPT)))
    weights = lax.dynamic_slice_in_dim(widened, start % SPT, count, 1)
    cosine = jnp.cos(blade_angle)[:, None]
    sine = jnp.sin(blade_angle)[:, None]
    factor = jnp.where(
        offset_of[None, :] < 2 * INF,
        jnp.float32(1.0),
        jnp.where(offset_of[None, :] < 3 * INF, cosine, sine),
    )
    return jnp.where(
        sensor_turbine[:, None] == turbine_of[None, :], weights * factor, jnp.float32(0.0)
    )


def gather_col(local_rows):
    ncol = lax.axis_size("col")
    if ncol > 8:
        return lax.all_gather(local_rows, "col", axis=0, tiled=True)
    pieces = [local_rows]
    for step in range(1, ncol):
        perm = [(c, (c + step) % ncol) for c in range(ncol)]
        pieces.append(lax.ppermute(local_rows, "col", perm))
    stacked = jnp.stack(pieces, 0)
    order = (lax.axis_index("col") - jnp.arange(ncol)) % ncol
    return jnp.take(stacked, order, axis=0).reshape((-1,) + local_rows.shape[1:])


def split_bf16(x):
    high = lax.reduce_precision(x, exponent_bits=8, mantissa_bits=7)
    return high.astype(jnp.bfloat16), (x - high).astype(jnp.bfloat16)


def column_rows(local_rows, col_count):
    nrow = lax.axis_size("row")
    ncol = lax.axis_size("col")
    devices = nrow * ncol
    pieces = []
    for step in range(nrow):
        perm = [(d, ((d % nrow + step) % nrow) * ncol + d // nrow) for d in range(devices)]
        pieces.append(lax.ppermute(local_rows, ("row", "col"), perm))
    stacked = jnp.stack(pieces, 0)
    order = (lax.axis_index("row") - jnp.arange(nrow)) % nrow
    return jnp.take(stacked, order, axis=0).reshape((col_count,) + local_rows.shape[1:])


def coupling_matrix(wake_block, upstream, turbine):
    slots = upstream[turbine]
    blocks = jnp.zeros((INF, TURB, INF), jnp.bfloat16)
    for slot_index in range(NUP):
        anchor = slots[slot_index]
        hit = (jnp.arange(TURB) == anchor)[None, :, None]
        blocks = blocks + jnp.where(
            hit, wake_block[turbine, slot_index][:, None, :], jnp.zeros((), jnp.bfloat16)
        )
    return blocks.reshape(INF, TURB * INF)


def mm(a, b):
    return jnp.dot(a, b, precision=lax.Precision.HIGHEST)


def cholesky_inverse(symmetric):
    size = symmetric.shape[0]
    block = 128 if size % 128 == 0 else size
    count = size // block
    eye = jnp.eye(block, dtype=jnp.float32)
    work = {
        (i, j): symmetric[i * block : (i + 1) * block, j * block : (j + 1) * block]
        for i in range(count)
        for j in range(i + 1)
    }
    lower = {}
    diag_inverse = {}
    for k in range(count):
        lower[k, k] = jnp.linalg.cholesky(work[k, k])
        diag_inverse[k] = jax.scipy.linalg.solve_triangular(lower[k, k], eye, lower=True)
        for i in range(k + 1, count):
            lower[i, k] = mm(work[i, k], diag_inverse[k].T)
        for i in range(k + 1, count):
            for j in range(k + 1, i + 1):
                work[i, j] = work[i, j] - mm(lower[i, k], lower[j, k].T)
    inv = {}
    for i in range(count):
        inv[i, i] = diag_inverse[i]
        for j in range(i - 1, -1, -1):
            total = sum(mm(lower[i, m], inv[m, j]) for m in range(j, i))
            inv[i, j] = -mm(diag_inverse[i], total)
    zero = jnp.zeros((block, block), jnp.float32)
    lower_inverse = jnp.block(
        [[inv[i, j] if j <= i else zero for j in range(count)] for i in range(count)]
    )
    return mm(lower_inverse.T, lower_inverse)


def dot_f32(a, b, dims):
    return lax.dot_general(a, b, (dims, ((), ())), preferred_element_type=jnp.float32)


def shards(
    covariance,
    self_block,
    wake_block,
    upstream,
    process_noise,
    sensor_turbine,
    azimuth_index,
    sensor_weight,
    sensor_noise,
):
    row_count, col_count = covariance.shape
    row_start = lax.axis_index("row") * row_count
    col_start = lax.axis_index("col") * col_count
    per_row = row_count // SPT
    per_col = max(1, col_count // SPT)
    first_turbine = lax.axis_index("row") * per_row

    cov3 = covariance.reshape(per_row, SPT, col_count)
    inflow_part = cov3[:, :INF, :].astype(jnp.bfloat16)
    inflow_all = lax.all_gather(inflow_part, "row", axis=0, tiled=True)
    inflow_all = inflow_all.reshape(TURB * INF, col_count)
    own_rows = gather_col(self_block)
    cov_high, cov_low = split_bf16(cov3)
    blocks = []
    for local in range(per_row):
        turbine = first_turbine + local
        diag_rows = own_rows[local * SPT : (local + 1) * SPT]
        result = dot_f32(diag_rows, cov_high[local], ((1,), (0,))) + dot_f32(
            diag_rows, cov_low[local], ((1,), (0,))
        )
        coupling = coupling_matrix(wake_block, upstream, turbine)
        inflow_sum = dot_f32(coupling, inflow_all, ((1,), (0,)))
        result = jnp.concatenate([result[:INF] + inflow_sum, result[INF:]], 0)
        blocks.append(result.astype(jnp.bfloat16))
    half_product = jnp.concatenate(blocks, 0)

    if col_count >= SPT:
        half3 = half_product.reshape(row_count, per_col, SPT)
        half_inflow = jnp.transpose(half3[:, :, :INF], (1, 0, 2))
        half_inflow_all = lax.all_gather(half_inflow, "col", axis=0, tiled=True)
        turbine_cols = [half3[:, local, :] for local in range(per_col)]
    else:
        full = lax.all_gather(half_product, "col", axis=1, tiled=True)
        half_inflow_all = jnp.transpose(full.reshape(row_count, TURB, SPT)[:, :, :INF], (1, 0, 2))
        turbine_cols = [lax.dynamic_slice_in_dim(full, (col_start // SPT) * SPT, SPT, 1)]
    target_rows = column_rows(self_block, col_count)
    piece_width = min(col_count, SPT)
    self_parts = []
    wake_parts = []
    for local in range(per_col):
        turbine = col_start // SPT + local
        diag_rows = target_rows[local * piece_width : (local + 1) * piece_width]
        result = lax.optimization_barrier(dot_f32(turbine_cols[local], diag_rows, ((1,), (1,))))
        coupling = coupling_matrix(wake_block, upstream, turbine).reshape(INF, TURB, INF)
        inflow_sum = dot_f32(half_inflow_all, coupling, ((0, 2), (1, 2)))
        inflow_sum = jnp.where(col_start % SPT == 0, inflow_sum, jnp.float32(0.0))
        self_parts.append(result)
        wake_parts.append(inflow_sum)
    row_ids = row_start + jnp.arange(row_count)
    col_ids = col_start + jnp.arange(col_count)
    self_full = jnp.concatenate(self_parts, 1) + jnp.where(
        row_ids[:, None] == col_ids[None, :], process_noise[None, :], jnp.float32(0.0)
    )
    padding = jnp.zeros((row_count, piece_width - INF), jnp.float32)
    wake_full = jnp.concatenate(
        [part for wake in wake_parts for part in (wake, padding)], 1
    )
    predicted = lax.optimization_barrier(self_full + wake_full)

    col_observe = observe_columns(
        sensor_weight, sensor_turbine, azimuth_index, col_start, col_count
    )
    partial_cross = jnp.dot(self_full, col_observe.T, precision=lax.Precision.HIGH)
    for local in range(per_col):
        start = local * piece_width
        partial_cross = partial_cross + jnp.dot(
            wake_parts[local], col_observe[:, start : start + INF].T, precision=lax.Precision.HIGH
        )
    cross_cov = lax.psum(partial_cross, "col")
    row_observe = observe_columns(
        sensor_weight, sensor_turbine, azimuth_index, row_start, row_count
    )
    partial_innovation = jnp.dot(row_observe, cross_cov, precision=lax.Precision.HIGH)
    innovation = lax.psum(partial_innovation, "row") + jnp.diag(sensor_noise)
    symmetric = 0.5 * (innovation + innovation.T)
    inverse = cholesky_inverse(symmetric)
    gain_block = jnp.dot(cross_cov, inverse, precision=lax.Precision.HIGH)
    piece = self_block.shape[0]
    own_piece = lax.dynamic_slice_in_dim(cross_cov, lax.axis_index("col") * piece, piece, 0)
    own_piece, innovation = lax.optimization_barrier((own_piece, innovation))
    target_cross = column_rows(own_piece, col_count)
    posterior = predicted - jnp.dot(gain_block, target_cross.T, precision=lax.Precision.HIGH)
    share = gain_block.shape[1] // lax.axis_size("col")
    gain_share = lax.dynamic_slice_in_dim(gain_block, lax.axis_index("col") * share, share, 1)
    return (posterior, gain_share)


def solution(mesh):
    in_specs = (P("row", "col"), P(("row", "col"), None), P(), P(), P("col"), P(), P(), P(), P())
    out_specs = (P("row", "col"), P("row", "col"))
    return jax.shard_map(shards, mesh=mesh, in_specs=in_specs, out_specs=out_specs, check_vma=False)
```

```python
import math

import jax
import jax.numpy as jnp
from jax import lax
from jax.sharding import PartitionSpec as P

TURB = 16
SPT = 512
INF = 128
NUP = 4
NAZ = 72


def broadcast(value, axis, root):
    mine = lax.axis_index(axis) == root
    return lax.psum(jnp.where(mine, value, jnp.zeros_like(value)), axis)


def observe_columns(sensor_weight, sensor_turbine, azimuth_index, start, count):
    sensors = sensor_weight.shape[0]
    matches = sensor_turbine[:, None] == jnp.arange(TURB)[None, :]
    rotor_index = jnp.sum(jnp.where(matches, azimuth_index[None, :], 0), axis=1)
    sensor_index = jnp.arange(sensors)
    blade_angle = rotor_index.astype(jnp.float32) * jnp.float32(2.0 * math.pi / NAZ) + (
        sensor_index % 3
    ).astype(jnp.float32) * jnp.float32(2.0 * math.pi / 3.0)
    positions = start + jnp.arange(count)
    turbine_of = positions // SPT
    offset_of = positions % SPT
    widened = jnp.tile(sensor_weight, (1, max(1, count // SPT)))
    weights = lax.dynamic_slice_in_dim(widened, start % SPT, count, 1)
    cosine = jnp.cos(blade_angle)[:, None]
    sine = jnp.sin(blade_angle)[:, None]
    factor = jnp.where(
        offset_of[None, :] < 2 * INF,
        jnp.float32(1.0),
        jnp.where(offset_of[None, :] < 3 * INF, cosine, sine),
    )
    return jnp.where(
        sensor_turbine[:, None] == turbine_of[None, :], weights * factor, jnp.float32(0.0)
    )


def gather_col(local_rows):
    ncol = lax.axis_size("col")
    if ncol > 8:
        return lax.all_gather(local_rows, "col", axis=0, tiled=True)
    pieces = [local_rows]
    for step in range(1, ncol):
        perm = [(c, (c + step) % ncol) for c in range(ncol)]
        pieces.append(lax.ppermute(local_rows, "col", perm))
    stacked = jnp.stack(pieces, 0)
    order = (lax.axis_index("col") - jnp.arange(ncol)) % ncol
    return jnp.take(stacked, order, axis=0).reshape((-1,) + local_rows.shape[1:])


def split_bf16(x):
    high = lax.reduce_precision(x, exponent_bits=8, mantissa_bits=7)
    return high.astype(jnp.bfloat16), (x - high).astype(jnp.bfloat16)


def column_rows(local_rows, col_count):
    nrow = lax.axis_size("row")
    ncol = lax.axis_size("col")
    devices = nrow * ncol
    pieces = []
    for step in range(nrow):
        perm = [(d, ((d % nrow + step) % nrow) * ncol + d // nrow) for d in range(devices)]
        pieces.append(lax.ppermute(local_rows, ("row", "col"), perm))
    stacked = jnp.stack(pieces, 0)
    order = (lax.axis_index("row") - jnp.arange(nrow)) % nrow
    return jnp.take(stacked, order, axis=0).reshape((col_count,) + local_rows.shape[1:])


def coupling_matrix(wake_block, upstream, turbine):
    slots = upstream[turbine]
    blocks = jnp.zeros((INF, TURB, INF), jnp.bfloat16)
    for slot_index in range(NUP):
        anchor = slots[slot_index]
        hit = (jnp.arange(TURB) == anchor)[None, :, None]
        blocks = blocks + jnp.where(
            hit, wake_block[turbine, slot_index][:, None, :], jnp.zeros((), jnp.bfloat16)
        )
    return blocks.reshape(INF, TURB * INF)


def mm(a, b):
    return jnp.dot(a, b, precision=lax.Precision.HIGHEST)


def cholesky_inverse(symmetric):
    size = symmetric.shape[0]
    block = 128 if size % 128 == 0 else size
    count = size // block
    eye = jnp.eye(block, dtype=jnp.float32)
    work = {
        (i, j): symmetric[i * block : (i + 1) * block, j * block : (j + 1) * block]
        for i in range(count)
        for j in range(i + 1)
    }
    lower = {}
    diag_inverse = {}
    for k in range(count):
        lower[k, k] = jnp.linalg.cholesky(work[k, k])
        diag_inverse[k] = jax.scipy.linalg.solve_triangular(lower[k, k], eye, lower=True)
        for i in range(k + 1, count):
            lower[i, k] = mm(work[i, k], diag_inverse[k].T)
        for i in range(k + 1, count):
            for j in range(k + 1, i + 1):
                work[i, j] = work[i, j] - mm(lower[i, k], lower[j, k].T)
    inv = {}
    for i in range(count):
        inv[i, i] = diag_inverse[i]
        for j in range(i - 1, -1, -1):
            total = sum(mm(lower[i, m], inv[m, j]) for m in range(j, i))
            inv[i, j] = -mm(diag_inverse[i], total)
    zero = jnp.zeros((block, block), jnp.float32)
    lower_inverse = jnp.block(
        [[inv[i, j] if j <= i else zero for j in range(count)] for i in range(count)]
    )
    return mm(lower_inverse.T, lower_inverse)


def dot_f32(a, b, dims):
    return lax.dot_general(a, b, (dims, ((), ())), preferred_element_type=jnp.float32)


def shards(
    covariance,
    self_block,
    wake_block,
    upstream,
    process_noise,
    sensor_turbine,
    azimuth_index,
    sensor_weight,
    sensor_noise,
):
    row_count, col_count = covariance.shape
    row_start = lax.axis_index("row") * row_count
    col_start = lax.axis_index("col") * col_count
    per_row = row_count // SPT
    per_col = max(1, col_count // SPT)
    first_turbine = lax.axis_index("row") * per_row

    cov3 = covariance.reshape(per_row, SPT, col_count)
    inflow_part = cov3[:, :INF, :].astype(jnp.bfloat16)
    inflow_all = lax.all_gather(inflow_part, "row", axis=0, tiled=True)
    inflow_all = inflow_all.reshape(TURB * INF, col_count)
    own_rows = gather_col(self_block)
    cov_high, cov_low = split_bf16(cov3)
    blocks = []
    for local in range(per_row):
        turbine = first_turbine + local
        diag_rows = own_rows[local * SPT : (local + 1) * SPT]
        result = dot_f32(diag_rows, cov_high[local], ((1,), (0,))) + dot_f32(
            diag_rows, cov_low[local], ((1,), (0,))
        )
        coupling = coupling_matrix(wake_block, upstream, turbine)
        inflow_sum = dot_f32(coupling, inflow_all, ((1,), (0,)))
        result = jnp.concatenate([result[:INF] + inflow_sum, result[INF:]], 0)
        blocks.append(result.astype(jnp.bfloat16))
    half_product = jnp.concatenate(blocks, 0)

    if col_count >= SPT:
        half3 = half_product.reshape(row_count, per_col, SPT)
        half_inflow = jnp.transpose(half3[:, :, :INF], (1, 0, 2))
        half_inflow_all = lax.all_gather(half_inflow, "col", axis=0, tiled=True)
        turbine_cols = [half3[:, local, :] for local in range(per_col)]
    else:
        full = lax.all_gather(half_product, "col", axis=1, tiled=True)
        half_inflow_all = jnp.transpose(full.reshape(row_count, TURB, SPT)[:, :, :INF], (1, 0, 2))
        turbine_cols = [lax.dynamic_slice_in_dim(full, (col_start // SPT) * SPT, SPT, 1)]
    target_rows = column_rows(self_block, col_count)
    piece_width = min(col_count, SPT)
    self_parts = []
    wake_parts = []
    for local in range(per_col):
        turbine = col_start // SPT + local
        diag_rows = target_rows[local * piece_width : (local + 1) * piece_width]
        result = lax.optimization_barrier(dot_f32(turbine_cols[local], diag_rows, ((1,), (1,))))
        coupling = coupling_matrix(wake_block, upstream, turbine).reshape(INF, TURB, INF)
        inflow_sum = dot_f32(half_inflow_all, coupling, ((0, 2), (1, 2)))
        inflow_sum = jnp.where(col_start % SPT == 0, inflow_sum, jnp.float32(0.0))
        self_parts.append(result)
        wake_parts.append(inflow_sum)
    row_ids = row_start + jnp.arange(row_count)
    col_ids = col_start + jnp.arange(col_count)
    self_full = jnp.concatenate(self_parts, 1) + jnp.where(
        row_ids[:, None] == col_ids[None, :], process_noise[None, :], jnp.float32(0.0)
    )
    padding = jnp.zeros((row_count, piece_width - INF), jnp.float32)
    wake_full = jnp.concatenate(
        [part for wake in wake_parts for part in (wake, padding)], 1
    )
    predicted = lax.optimization_barrier(self_full + wake_full)

    col_observe = observe_columns(
        sensor_weight, sensor_turbine, azimuth_index, col_start, col_count
    )
    partial_cross = jnp.dot(self_full, col_observe.T, precision=lax.Precision.HIGH)
    for local in range(per_col):
        start = local * piece_width
        partial_cross = partial_cross + jnp.dot(
            wake_parts[local], col_observe[:, start : start + INF].T, precision=lax.Precision.HIGH
        )
    cross_piece = lax.psum_scatter(partial_cross, "col", scatter_dimension=0, tiled=True)
    target_cross = column_rows(cross_piece, col_count)
    cross_cov = lax.all_gather(cross_piece, "col", axis=0, tiled=True)
    row_observe = observe_columns(
        sensor_weight, sensor_turbine, azimuth_index, row_start, row_count
    )
    partial_innovation = jnp.dot(row_observe, cross_cov, precision=lax.Precision.HIGH)
    innovation = lax.psum(partial_innovation, "row") + jnp.diag(sensor_noise)
    symmetric = 0.5 * (innovation + innovation.T)
    inverse = cholesky_inverse(symmetric)
    gain_block = jnp.dot(cross_cov, inverse, precision=lax.Precision.HIGH)
    posterior = predicted - jnp.dot(gain_block, target_cross.T, precision=lax.Precision.HIGH)
    share = gain_block.shape[1] // lax.axis_size("col")
    gain_share = lax.dynamic_slice_in_dim(gain_block, lax.axis_index("col") * share, share, 1)
    return (posterior, gain_share)


def solution(mesh):
    in_specs = (P("row", "col"), P(("row", "col"), None), P(), P(), P("col"), P(), P(), P(), P())
    out_specs = (P("row", "col"), P("row", "col"))
    return jax.shard_map(shards, mesh=mesh, in_specs=in_specs, out_specs=out_specs, check_vma=False)
```

```python
import math

import jax
import jax.numpy as jnp
from jax import lax
from jax.sharding import PartitionSpec as P

TURB = 16
SPT = 512
INF = 128
NUP = 4
NAZ = 72


def broadcast(value, axis, root):
    mine = lax.axis_index(axis) == root
    return lax.psum(jnp.where(mine, value, jnp.zeros_like(value)), axis)


def observe_columns(sensor_weight, sensor_turbine, azimuth_index, start, count):
    sensors = sensor_weight.shape[0]
    matches = sensor_turbine[:, None] == jnp.arange(TURB)[None, :]
    rotor_index = jnp.sum(jnp.where(matches, azimuth_index[None, :], 0), axis=1)
    sensor_index = jnp.arange(sensors)
    blade_angle = rotor_index.astype(jnp.float32) * jnp.float32(2.0 * math.pi / NAZ) + (
        sensor_index % 3
    ).astype(jnp.float32) * jnp.float32(2.0 * math.pi / 3.0)
    positions = start + jnp.arange(count)
    turbine_of = positions // SPT
    offset_of = positions % SPT
    widened = jnp.tile(sensor_weight, (1, max(1, count // SPT)))
    weights = lax.dynamic_slice_in_dim(widened, start % SPT, count, 1)
    cosine = jnp.cos(blade_angle)[:, None]
    sine = jnp.sin(blade_angle)[:, None]
    factor = jnp.where(
        offset_of[None, :] < 2 * INF,
        jnp.float32(1.0),
        jnp.where(offset_of[None, :] < 3 * INF, cosine, sine),
    )
    return jnp.where(
        sensor_turbine[:, None] == turbine_of[None, :], weights * factor, jnp.float32(0.0)
    )


def gather_col(local_rows):
    ncol = lax.axis_size("col")
    if ncol > 8:
        return lax.all_gather(local_rows, "col", axis=0, tiled=True)
    pieces = [local_rows]
    for step in range(1, ncol):
        perm = [(c, (c + step) % ncol) for c in range(ncol)]
        pieces.append(lax.ppermute(local_rows, "col", perm))
    stacked = jnp.stack(pieces, 0)
    order = (lax.axis_index("col") - jnp.arange(ncol)) % ncol
    return jnp.take(stacked, order, axis=0).reshape((-1,) + local_rows.shape[1:])


def split_bf16(x):
    high = lax.reduce_precision(x, exponent_bits=8, mantissa_bits=7)
    return high.astype(jnp.bfloat16), (x - high).astype(jnp.bfloat16)


def column_rows(local_rows, col_count):
    nrow = lax.axis_size("row")
    ncol = lax.axis_size("col")
    devices = nrow * ncol
    pieces = []
    for step in range(nrow):
        perm = [(d, ((d % nrow + step) % nrow) * ncol + d // nrow) for d in range(devices)]
        pieces.append(lax.ppermute(local_rows, ("row", "col"), perm))
    stacked = jnp.stack(pieces, 0)
    order = (lax.axis_index("row") - jnp.arange(nrow)) % nrow
    return jnp.take(stacked, order, axis=0).reshape((col_count,) + local_rows.shape[1:])


def coupling_matrix(wake_block, upstream, turbine):
    slots = upstream[turbine]
    blocks = jnp.zeros((INF, TURB, INF), jnp.bfloat16)
    for slot_index in range(NUP):
        anchor = slots[slot_index]
        hit = (jnp.arange(TURB) == anchor)[None, :, None]
        blocks = blocks + jnp.where(
            hit, wake_block[turbine, slot_index][:, None, :], jnp.zeros((), jnp.bfloat16)
        )
    return blocks.reshape(INF, TURB * INF)


def sum_symmetric(value, axis):
    size = value.shape[0]
    block = 128 if size % 128 == 0 else size
    count = size // block
    pairs = [(i, j) for i in range(count) for j in range(i + 1)]
    lower = jnp.stack(
        [value[i * block : (i + 1) * block, j * block : (j + 1) * block] for i, j in pairs], 0
    )
    lower = lax.psum(lower, axis)
    found = dict(zip(pairs, range(len(pairs))))
    rows = []
    for i in range(count):
        rows.append(
            jnp.concatenate(
                [lower[found[i, j]] if j <= i else lower[found[j, i]].T for j in range(count)], 1
            )
        )
    return jnp.concatenate(rows, 0)


def mm(a, b):
    return jnp.dot(a, b, precision=lax.Precision.HIGHEST)


def cholesky_inverse(symmetric):
    size = symmetric.shape[0]
    block = 128 if size % 128 == 0 else size
    count = size // block
    eye = jnp.eye(block, dtype=jnp.float32)
    work = {
        (i, j): symmetric[i * block : (i + 1) * block, j * block : (j + 1) * block]
        for i in range(count)
        for j in range(i + 1)
    }
    lower = {}
    diag_inverse = {}
    for k in range(count):
        lower[k, k] = jnp.linalg.cholesky(work[k, k])
        diag_inverse[k] = jax.scipy.linalg.solve_triangular(lower[k, k], eye, lower=True)
        for i in range(k + 1, count):
            lower[i, k] = mm(work[i, k], diag_inverse[k].T)
        for i in range(k + 1, count):
            for j in range(k + 1, i + 1):
                work[i, j] = work[i, j] - mm(lower[i, k], lower[j, k].T)
    inv = {}
    for i in range(count):
        inv[i, i] = diag_inverse[i]
        for j in range(i - 1, -1, -1):
            total = sum(mm(lower[i, m], inv[m, j]) for m in range(j, i))
            inv[i, j] = -mm(diag_inverse[i], total)
    zero = jnp.zeros((block, block), jnp.float32)
    lower_inverse = jnp.block(
        [[inv[i, j] if j <= i else zero for j in range(count)] for i in range(count)]
    )
    return mm(lower_inverse.T, lower_inverse)


def dot_f32(a, b, dims):
    return lax.dot_general(a, b, (dims, ((), ())), preferred_element_type=jnp.float32)


def shards(
    covariance,
    self_block,
    wake_block,
    upstream,
    process_noise,
    sensor_turbine,
    azimuth_index,
    sensor_weight,
    sensor_noise,
):
    row_count, col_count = covariance.shape
    row_start = lax.axis_index("row") * row_count
    col_start = lax.axis_index("col") * col_count
    per_row = row_count // SPT
    per_col = max(1, col_count // SPT)
    first_turbine = lax.axis_index("row") * per_row

    cov3 = covariance.reshape(per_row, SPT, col_count)
    inflow_part = cov3[:, :INF, :].astype(jnp.bfloat16)
    inflow_all = lax.all_gather(inflow_part, "row", axis=0, tiled=True)
    inflow_all = inflow_all.reshape(TURB * INF, col_count)
    own_rows = gather_col(self_block)
    cov_high, cov_low = split_bf16(cov3)
    blocks = []
    for local in range(per_row):
        turbine = first_turbine + local
        diag_rows = own_rows[local * SPT : (local + 1) * SPT]
        result = dot_f32(diag_rows, cov_high[local], ((1,), (0,))) + dot_f32(
            diag_rows, cov_low[local], ((1,), (0,))
        )
        coupling = coupling_matrix(wake_block, upstream, turbine)
        inflow_sum = dot_f32(coupling, inflow_all, ((1,), (0,)))
        result = jnp.concatenate([result[:INF] + inflow_sum, result[INF:]], 0)
        blocks.append(result.astype(jnp.bfloat16))
    half_product = jnp.concatenate(blocks, 0)

    if col_count >= SPT:
        half3 = half_product.reshape(row_count, per_col, SPT)
        half_inflow = jnp.transpose(half3[:, :, :INF], (1, 0, 2))
        half_inflow_all = lax.all_gather(half_inflow, "col", axis=0, tiled=True)
        turbine_cols = [half3[:, local, :] for local in range(per_col)]
    else:
        full = lax.all_gather(half_product, "col", axis=1, tiled=True)
        half_inflow_all = jnp.transpose(full.reshape(row_count, TURB, SPT)[:, :, :INF], (1, 0, 2))
        turbine_cols = [lax.dynamic_slice_in_dim(full, (col_start // SPT) * SPT, SPT, 1)]
    target_rows = column_rows(self_block, col_count)
    piece_width = min(col_count, SPT)
    self_parts = []
    wake_parts = []
    for local in range(per_col):
        turbine = col_start // SPT + local
        diag_rows = target_rows[local * piece_width : (local + 1) * piece_width]
        result = lax.optimization_barrier(dot_f32(turbine_cols[local], diag_rows, ((1,), (1,))))
        coupling = coupling_matrix(wake_block, upstream, turbine).reshape(INF, TURB, INF)
        inflow_sum = dot_f32(half_inflow_all, coupling, ((0, 2), (1, 2)))
        inflow_sum = jnp.where(col_start % SPT == 0, inflow_sum, jnp.float32(0.0))
        self_parts.append(result)
        wake_parts.append(inflow_sum)
    row_ids = row_start + jnp.arange(row_count)
    col_ids = col_start + jnp.arange(col_count)
    self_full = jnp.concatenate(self_parts, 1) + jnp.where(
        row_ids[:, None] == col_ids[None, :], process_noise[None, :], jnp.float32(0.0)
    )
    padding = jnp.zeros((row_count, piece_width - INF), jnp.float32)
    wake_full = jnp.concatenate(
        [part for wake in wake_parts for part in (wake, padding)], 1
    )
    predicted = lax.optimization_barrier(self_full + wake_full)

    col_observe = observe_columns(
        sensor_weight, sensor_turbine, azimuth_index, col_start, col_count
    )
    partial_cross = jnp.dot(self_full, col_observe.T, precision=lax.Precision.HIGH)
    for local in range(per_col):
        start = local * piece_width
        partial_cross = partial_cross + jnp.dot(
            wake_parts[local], col_observe[:, start : start + INF].T, precision=lax.Precision.HIGH
        )
    cross_cov = lax.psum(partial_cross, "col")
    row_observe = observe_columns(
        sensor_weight, sensor_turbine, azimuth_index, row_start, row_count
    )
    partial_innovation = jnp.dot(row_observe, cross_cov, precision=lax.Precision.HIGH)
    symmetric = sum_symmetric(0.5 * (partial_innovation + partial_innovation.T), "row")
    symmetric = symmetric + jnp.diag(sensor_noise)
    inverse = cholesky_inverse(symmetric)
    gain_block = jnp.dot(cross_cov, inverse, precision=lax.Precision.HIGH)
    piece = self_block.shape[0]
    own_piece = lax.dynamic_slice_in_dim(cross_cov, lax.axis_index("col") * piece, piece, 0)
    own_piece, symmetric = lax.optimization_barrier((own_piece, symmetric))
    target_cross = column_rows(own_piece, col_count)
    posterior = predicted - jnp.dot(gain_block, target_cross.T, precision=lax.Precision.HIGH)
    share = gain_block.shape[1] // lax.axis_size("col")
    gain_share = lax.dynamic_slice_in_dim(gain_block, lax.axis_index("col") * share, share, 1)
    return (posterior, gain_share)


def solution(mesh):
    in_specs = (P("row", "col"), P(("row", "col"), None), P(), P(), P("col"), P(), P(), P(), P())
    out_specs = (P("row", "col"), P("row", "col"))
    return jax.shard_map(shards, mesh=mesh, in_specs=in_specs, out_specs=out_specs, check_vma=False)
```

```python
import math

import jax
import jax.numpy as jnp
from jax import lax
from jax.sharding import PartitionSpec as P

TURB = 16
SPT = 512
INF = 128
NUP = 4
NAZ = 72


def broadcast(value, axis, root):
    mine = lax.axis_index(axis) == root
    return lax.psum(jnp.where(mine, value, jnp.zeros_like(value)), axis)


def observe_columns(sensor_weight, sensor_turbine, azimuth_index, start, count):
    sensors = sensor_weight.shape[0]
    matches = sensor_turbine[:, None] == jnp.arange(TURB)[None, :]
    rotor_index = jnp.sum(jnp.where(matches, azimuth_index[None, :], 0), axis=1)
    sensor_index = jnp.arange(sensors)
    blade_angle = rotor_index.astype(jnp.float32) * jnp.float32(2.0 * math.pi / NAZ) + (
        sensor_index % 3
    ).astype(jnp.float32) * jnp.float32(2.0 * math.pi / 3.0)
    positions = start + jnp.arange(count)
    turbine_of = positions // SPT
    offset_of = positions % SPT
    widened = jnp.tile(sensor_weight, (1, max(1, count // SPT)))
    weights = lax.dynamic_slice_in_dim(widened, start % SPT, count, 1)
    cosine = jnp.cos(blade_angle)[:, None]
    sine = jnp.sin(blade_angle)[:, None]
    factor = jnp.where(
        offset_of[None, :] < 2 * INF,
        jnp.float32(1.0),
        jnp.where(offset_of[None, :] < 3 * INF, cosine, sine),
    )
    return jnp.where(
        sensor_turbine[:, None] == turbine_of[None, :], weights * factor, jnp.float32(0.0)
    )


def gather_col(local_rows):
    ncol = lax.axis_size("col")
    if ncol > 8:
        return lax.all_gather(local_rows, "col", axis=0, tiled=True)
    pieces = [local_rows]
    for step in range(1, ncol):
        perm = [(c, (c + step) % ncol) for c in range(ncol)]
        pieces.append(lax.ppermute(local_rows, "col", perm))
    stacked = jnp.stack(pieces, 0)
    order = (lax.axis_index("col") - jnp.arange(ncol)) % ncol
    return jnp.take(stacked, order, axis=0).reshape((-1,) + local_rows.shape[1:])


def split_bf16(x):
    high = lax.reduce_precision(x, exponent_bits=8, mantissa_bits=7)
    return high.astype(jnp.bfloat16), (x - high).astype(jnp.bfloat16)


def column_rows(local_rows, col_count):
    nrow = lax.axis_size("row")
    ncol = lax.axis_size("col")
    devices = nrow * ncol
    pieces = []
    for step in range(nrow):
        perm = [(d, ((d % nrow + step) % nrow) * ncol + d // nrow) for d in range(devices)]
        pieces.append(lax.ppermute(local_rows, ("row", "col"), perm))
    stacked = jnp.stack(pieces, 0)
    order = (lax.axis_index("row") - jnp.arange(nrow)) % nrow
    return jnp.take(stacked, order, axis=0).reshape((col_count,) + local_rows.shape[1:])


def coupling_matrix(wake_block, upstream, turbine):
    slots = upstream[turbine]
    blocks = jnp.zeros((INF, TURB, INF), jnp.bfloat16)
    for slot_index in range(NUP):
        anchor = slots[slot_index]
        hit = (jnp.arange(TURB) == anchor)[None, :, None]
        blocks = blocks + jnp.where(
            hit, wake_block[turbine, slot_index][:, None, :], jnp.zeros((), jnp.bfloat16)
        )
    return blocks.reshape(INF, TURB * INF)


def mm(a, b):
    return jnp.dot(a, b, precision=lax.Precision.HIGH)


def cholesky_inverse(symmetric):
    size = symmetric.shape[0]
    block = 128 if size % 128 == 0 else size
    count = size // block
    eye = jnp.eye(block, dtype=jnp.float32)
    work = {
        (i, j): symmetric[i * block : (i + 1) * block, j * block : (j + 1) * block]
        for i in range(count)
        for j in range(i + 1)
    }
    lower = {}
    diag_inverse = {}
    for k in range(count):
        lower[k, k] = jnp.linalg.cholesky(work[k, k])
        diag_inverse[k] = jax.scipy.linalg.solve_triangular(lower[k, k], eye, lower=True)
        for i in range(k + 1, count):
            lower[i, k] = mm(work[i, k], diag_inverse[k].T)
        for i in range(k + 1, count):
            for j in range(k + 1, i + 1):
                work[i, j] = work[i, j] - mm(lower[i, k], lower[j, k].T)
    inv = {}
    for i in range(count):
        inv[i, i] = diag_inverse[i]
        for j in range(i - 1, -1, -1):
            total = sum(mm(lower[i, m], inv[m, j]) for m in range(j, i))
            inv[i, j] = -mm(diag_inverse[i], total)
    zero = jnp.zeros((block, block), jnp.float32)
    lower_inverse = jnp.block(
        [[inv[i, j] if j <= i else zero for j in range(count)] for i in range(count)]
    )
    return mm(lower_inverse.T, lower_inverse)


def dot_f32(a, b, dims):
    return lax.dot_general(a, b, (dims, ((), ())), preferred_element_type=jnp.float32)


def shards(
    covariance,
    self_block,
    wake_block,
    upstream,
    process_noise,
    sensor_turbine,
    azimuth_index,
    sensor_weight,
    sensor_noise,
):
    row_count, col_count = covariance.shape
    row_start = lax.axis_index("row") * row_count
    col_start = lax.axis_index("col") * col_count
    per_row = row_count // SPT
    per_col = max(1, col_count // SPT)
    first_turbine = lax.axis_index("row") * per_row

    cov3 = covariance.reshape(per_row, SPT, col_count)
    inflow_part = cov3[:, :INF, :].astype(jnp.bfloat16)
    inflow_all = lax.all_gather(inflow_part, "row", axis=0, tiled=True)
    inflow_all = inflow_all.reshape(TURB * INF, col_count)
    own_rows = gather_col(self_block)
    cov_high, cov_low = split_bf16(cov3)
    blocks = []
    for local in range(per_row):
        turbine = first_turbine + local
        diag_rows = own_rows[local * SPT : (local + 1) * SPT]
        result = dot_f32(diag_rows, cov_high[local], ((1,), (0,))) + dot_f32(
            diag_rows, cov_low[local], ((1,), (0,))
        )
        coupling = coupling_matrix(wake_block, upstream, turbine)
        inflow_sum = dot_f32(coupling, inflow_all, ((1,), (0,)))
        result = jnp.concatenate([result[:INF] + inflow_sum, result[INF:]], 0)
        blocks.append(result.astype(jnp.bfloat16))
    half_product = jnp.concatenate(blocks, 0)

    if col_count >= SPT:
        half3 = half_product.reshape(row_count, per_col, SPT)
        half_inflow = jnp.transpose(half3[:, :, :INF], (1, 0, 2))
        half_inflow_all = lax.all_gather(half_inflow, "col", axis=0, tiled=True)
        turbine_cols = [half3[:, local, :] for local in range(per_col)]
    else:
        full = lax.all_gather(half_product, "col", axis=1, tiled=True)
        half_inflow_all = jnp.transpose(full.reshape(row_count, TURB, SPT)[:, :, :INF], (1, 0, 2))
        turbine_cols = [lax.dynamic_slice_in_dim(full, (col_start // SPT) * SPT, SPT, 1)]
    target_rows = column_rows(self_block, col_count)
    piece_width = min(col_count, SPT)
    self_parts = []
    wake_parts = []
    for local in range(per_col):
        turbine = col_start // SPT + local
        diag_rows = target_rows[local * piece_width : (local + 1) * piece_width]
        result = lax.optimization_barrier(dot_f32(turbine_cols[local], diag_rows, ((1,), (1,))))
        coupling = coupling_matrix(wake_block, upstream, turbine).reshape(INF, TURB, INF)
        inflow_sum = dot_f32(half_inflow_all, coupling, ((0, 2), (1, 2)))
        inflow_sum = jnp.where(col_start % SPT == 0, inflow_sum, jnp.float32(0.0))
        self_parts.append(result)
        wake_parts.append(inflow_sum)
    row_ids = row_start + jnp.arange(row_count)
    col_ids = col_start + jnp.arange(col_count)
    self_full = jnp.concatenate(self_parts, 1) + jnp.where(
        row_ids[:, None] == col_ids[None, :], process_noise[None, :], jnp.float32(0.0)
    )
    padding = jnp.zeros((row_count, piece_width - INF), jnp.float32)
    wake_full = jnp.concatenate(
        [part for wake in wake_parts for part in (wake, padding)], 1
    )
    predicted = lax.optimization_barrier(self_full + wake_full)

    col_observe = observe_columns(
        sensor_weight, sensor_turbine, azimuth_index, col_start, col_count
    )
    partial_cross = jnp.dot(self_full, col_observe.T, precision=lax.Precision.HIGH)
    for local in range(per_col):
        start = local * piece_width
        partial_cross = partial_cross + jnp.dot(
            wake_parts[local], col_observe[:, start : start + INF].T, precision=lax.Precision.HIGH
        )
    cross_cov = lax.psum(partial_cross, "col")
    row_observe = observe_columns(
        sensor_weight, sensor_turbine, azimuth_index, row_start, row_count
    )
    partial_innovation = jnp.dot(row_observe, cross_cov, precision=lax.Precision.HIGH)
    innovation = lax.psum(partial_innovation, "row") + jnp.diag(sensor_noise)
    symmetric = 0.5 * (innovation + innovation.T)
    inverse = cholesky_inverse(symmetric)
    gain_block = jnp.dot(cross_cov, inverse, precision=lax.Precision.HIGH)
    piece = self_block.shape[0]
    own_piece = lax.dynamic_slice_in_dim(cross_cov, lax.axis_index("col") * piece, piece, 0)
    own_piece, innovation = lax.optimization_barrier((own_piece, innovation))
    target_cross = column_rows(own_piece, col_count)
    posterior = predicted - jnp.dot(gain_block, target_cross.T, precision=lax.Precision.HIGH)
    share = gain_block.shape[1] // lax.axis_size("col")
    gain_share = lax.dynamic_slice_in_dim(gain_block, lax.axis_index("col") * share, share, 1)
    return (posterior, gain_share)


def solution(mesh):
    in_specs = (P("row", "col"), P(("row", "col"), None), P(), P(), P("col"), P(), P(), P(), P())
    out_specs = (P("row", "col"), P("row", "col"))
    return jax.shard_map(shards, mesh=mesh, in_specs=in_specs, out_specs=out_specs, check_vma=False)
```

```python
import math

import jax
import jax.numpy as jnp
from jax import lax
from jax.sharding import PartitionSpec as P

TURB = 16
SPT = 512
INF = 128
NUP = 4
NAZ = 72


def broadcast(value, axis, root):
    mine = lax.axis_index(axis) == root
    return lax.psum(jnp.where(mine, value, jnp.zeros_like(value)), axis)


def observe_columns(sensor_weight, sensor_turbine, azimuth_index, start, count):
    sensors = sensor_weight.shape[0]
    matches = sensor_turbine[:, None] == jnp.arange(TURB)[None, :]
    rotor_index = jnp.sum(jnp.where(matches, azimuth_index[None, :], 0), axis=1)
    sensor_index = jnp.arange(sensors)
    blade_angle = rotor_index.astype(jnp.float32) * jnp.float32(2.0 * math.pi / NAZ) + (
        sensor_index % 3
    ).astype(jnp.float32) * jnp.float32(2.0 * math.pi / 3.0)
    positions = start + jnp.arange(count)
    turbine_of = positions // SPT
    offset_of = positions % SPT
    widened = jnp.tile(sensor_weight, (1, max(1, count // SPT)))
    weights = lax.dynamic_slice_in_dim(widened, start % SPT, count, 1)
    cosine = jnp.cos(blade_angle)[:, None]
    sine = jnp.sin(blade_angle)[:, None]
    factor = jnp.where(
        offset_of[None, :] < 2 * INF,
        jnp.float32(1.0),
        jnp.where(offset_of[None, :] < 3 * INF, cosine, sine),
    )
    return jnp.where(
        sensor_turbine[:, None] == turbine_of[None, :], weights * factor, jnp.float32(0.0)
    )


def gather_col(local_rows):
    ncol = lax.axis_size("col")
    if ncol > 8:
        return lax.all_gather(local_rows, "col", axis=0, tiled=True)
    pieces = [local_rows]
    for step in range(1, ncol):
        perm = [(c, (c + step) % ncol) for c in range(ncol)]
        pieces.append(lax.ppermute(local_rows, "col", perm))
    stacked = jnp.stack(pieces, 0)
    order = (lax.axis_index("col") - jnp.arange(ncol)) % ncol
    return jnp.take(stacked, order, axis=0).reshape((-1,) + local_rows.shape[1:])


def split_bf16(x):
    high = lax.reduce_precision(x, exponent_bits=8, mantissa_bits=7)
    return high.astype(jnp.bfloat16), (x - high).astype(jnp.bfloat16)


def column_rows(local_rows, col_count):
    nrow = lax.axis_size("row")
    ncol = lax.axis_size("col")
    devices = nrow * ncol
    pieces = []
    for step in range(nrow):
        perm = [(d, ((d % nrow + step) % nrow) * ncol + d // nrow) for d in range(devices)]
        pieces.append(lax.ppermute(local_rows, ("row", "col"), perm))
    stacked = jnp.stack(pieces, 0)
    order = (lax.axis_index("row") - jnp.arange(nrow)) % nrow
    return jnp.take(stacked, order, axis=0).reshape((col_count,) + local_rows.shape[1:])


def coupling_matrix(wake_block, upstream, turbine):
    slots = upstream[turbine]
    blocks = jnp.zeros((INF, TURB, INF), jnp.bfloat16)
    for slot_index in range(NUP):
        anchor = slots[slot_index]
        hit = (jnp.arange(TURB) == anchor)[None, :, None]
        blocks = blocks + jnp.where(
            hit, wake_block[turbine, slot_index][:, None, :], jnp.zeros((), jnp.bfloat16)
        )
    return blocks.reshape(INF, TURB * INF)


def mm(a, b):
    return jnp.dot(a, b, precision=lax.Precision.HIGH)


def cholesky_inverse(symmetric):
    size = symmetric.shape[0]
    block = 128 if size % 128 == 0 else size
    count = size // block
    eye = jnp.eye(block, dtype=jnp.float32)
    work = {
        (i, j): symmetric[i * block : (i + 1) * block, j * block : (j + 1) * block]
        for i in range(count)
        for j in range(i + 1)
    }
    lower = {}
    diag_inverse = {}
    for k in range(count):
        lower[k, k] = jnp.linalg.cholesky(work[k, k])
        diag_inverse[k] = jax.scipy.linalg.solve_triangular(lower[k, k], eye, lower=True)
        for i in range(k + 1, count):
            lower[i, k] = mm(work[i, k], diag_inverse[k].T)
        for i in range(k + 1, count):
            for j in range(k + 1, i + 1):
                work[i, j] = work[i, j] - mm(lower[i, k], lower[j, k].T)
    inv = {}
    for i in range(count):
        inv[i, i] = diag_inverse[i]
        for j in range(i - 1, -1, -1):
            total = sum(mm(lower[i, m], inv[m, j]) for m in range(j, i))
            inv[i, j] = -mm(diag_inverse[i], total)
    zero = jnp.zeros((block, block), jnp.float32)
    lower_inverse = jnp.block(
        [[inv[i, j] if j <= i else zero for j in range(count)] for i in range(count)]
    )
    return mm(lower_inverse.T, lower_inverse)


def dot_f32(a, b, dims):
    return lax.dot_general(a, b, (dims, ((), ())), preferred_element_type=jnp.float32)


def shards(
    covariance,
    self_block,
    wake_block,
    upstream,
    process_noise,
    sensor_turbine,
    azimuth_index,
    sensor_weight,
    sensor_noise,
):
    row_count, col_count = covariance.shape
    row_start = lax.axis_index("row") * row_count
    col_start = lax.axis_index("col") * col_count
    per_row = row_count // SPT
    per_col = max(1, col_count // SPT)
    first_turbine = lax.axis_index("row") * per_row

    cov3 = covariance.reshape(per_row, SPT, col_count)
    inflow_part = cov3[:, :INF, :].astype(jnp.bfloat16)
    inflow_all = lax.all_gather(inflow_part, "row", axis=0, tiled=True)
    inflow_all = inflow_all.reshape(TURB * INF, col_count)
    own_rows = gather_col(self_block)
    cov_high, cov_low = split_bf16(cov3)
    blocks = []
    for local in range(per_row):
        turbine = first_turbine + local
        diag_rows = own_rows[local * SPT : (local + 1) * SPT]
        result = dot_f32(diag_rows, cov_high[local], ((1,), (0,))) + dot_f32(
            diag_rows, cov_low[local], ((1,), (0,))
        )
        coupling = coupling_matrix(wake_block, upstream, turbine)
        inflow_sum = dot_f32(coupling, inflow_all, ((1,), (0,)))
        result = jnp.concatenate([result[:INF] + inflow_sum, result[INF:]], 0)
        blocks.append(result.astype(jnp.bfloat16))
    half_product = jnp.concatenate(blocks, 0)

    if col_count >= SPT:
        half3 = half_product.reshape(row_count, per_col, SPT)
        half_inflow = jnp.transpose(half3[:, :, :INF], (1, 0, 2))
        half_inflow_all = lax.all_gather(half_inflow, "col", axis=0, tiled=True)
        turbine_cols = [half3[:, local, :] for local in range(per_col)]
    else:
        full = lax.all_gather(half_product, "col", axis=1, tiled=True)
        half_inflow_all = jnp.transpose(full.reshape(row_count, TURB, SPT)[:, :, :INF], (1, 0, 2))
        turbine_cols = [lax.dynamic_slice_in_dim(full, (col_start // SPT) * SPT, SPT, 1)]
    target_rows = column_rows(self_block, col_count)
    piece_width = min(col_count, SPT)
    self_parts = []
    wake_parts = []
    for local in range(per_col):
        turbine = col_start // SPT + local
        diag_rows = target_rows[local * piece_width : (local + 1) * piece_width]
        result = lax.optimization_barrier(dot_f32(turbine_cols[local], diag_rows, ((1,), (1,))))
        coupling = coupling_matrix(wake_block, upstream, turbine).reshape(INF, TURB, INF)
        inflow_sum = dot_f32(half_inflow_all, coupling, ((0, 2), (1, 2)))
        inflow_sum = jnp.where(col_start % SPT == 0, inflow_sum, jnp.float32(0.0))
        self_parts.append(result)
        wake_parts.append(inflow_sum)
    row_ids = row_start + jnp.arange(row_count)
    col_ids = col_start + jnp.arange(col_count)
    self_full = jnp.concatenate(self_parts, 1) + jnp.where(
        row_ids[:, None] == col_ids[None, :], process_noise[None, :], jnp.float32(0.0)
    )
    padding = jnp.zeros((row_count, piece_width - INF), jnp.float32)
    wake_full = jnp.concatenate(
        [part for wake in wake_parts for part in (wake, padding)], 1
    )
    predicted = lax.optimization_barrier(self_full + wake_full)

    col_observe = observe_columns(
        sensor_weight, sensor_turbine, azimuth_index, col_start, col_count
    )
    partial_cross = jnp.dot(self_full, col_observe.T, precision=lax.Precision.HIGH)
    for local in range(per_col):
        start = local * piece_width
        partial_cross = partial_cross + jnp.dot(
            wake_parts[local], col_observe[:, start : start + INF].T, precision=lax.Precision.HIGH
        )
    cross_cov = lax.psum(partial_cross, "col")
    row_observe = observe_columns(
        sensor_weight, sensor_turbine, azimuth_index, row_start, row_count
    )
    partial_innovation = jnp.dot(row_observe, cross_cov, precision=lax.Precision.HIGH)
    innovation = lax.psum(partial_innovation, "row") + jnp.diag(sensor_noise)
    symmetric = 0.5 * (innovation + innovation.T)
    inverse = cholesky_inverse(symmetric)
    piece = self_block.shape[0]
    own_piece = lax.dynamic_slice_in_dim(cross_cov, lax.axis_index("col") * piece, piece, 0)
    own_piece, innovation = lax.optimization_barrier((own_piece, innovation))
    target_cross = column_rows(own_piece, col_count)
    projected = jnp.dot(inverse, target_cross.T, precision=lax.Precision.HIGH)
    posterior = predicted - jnp.dot(cross_cov, projected, precision=lax.Precision.HIGH)
    share = inverse.shape[1] // lax.axis_size("col")
    inverse_share = lax.dynamic_slice_in_dim(inverse, lax.axis_index("col") * share, share, 1)
    gain_share = jnp.dot(cross_cov, inverse_share, precision=lax.Precision.HIGH)
    return (posterior, gain_share)


def solution(mesh):
    in_specs = (P("row", "col"), P(("row", "col"), None), P(), P(), P("col"), P(), P(), P(), P())
    out_specs = (P("row", "col"), P("row", "col"))
    return jax.shard_map(shards, mesh=mesh, in_specs=in_specs, out_specs=out_specs, check_vma=False)
```
